32 devices in a mesh: ctx: 16 (over z, y, core), head: 2 (over x).
Axes of the slice: x: 2, y: 2, z: 4, core: 2. Of those that a mesh axis runs over, the one named last changes fastest.
Arguments:
- queries: bfloat16 [4096, 2048], P('ctx', 'head'), may hold values from -160 to 160
- key_rows: bfloat16 [4096, 128], P(('ctx', 'head')), may hold values from -9 to 9
- value_rows: bfloat16 [4096, 128], P(('ctx', 'head')), may hold values from -6 to 6
- span_order: int32 [32], replicated, may hold values from 0 to 31, as said below
- doc_start: int32 [4096], P('ctx'), may hold values from 0 to 3584, as said below
Outputs:
- attended: bfloat16 [4096, 2048], P('ctx', 'head')
The draws below stay inside these ranges and needn't reach their ends.
Inputs may be any that keep to these rules, and one draw needn't show every extreme that they name: `span_order`: each of 0 to 31 once; entries 2 d and 2 d + 1 are a span c and its mirror 32 - 1 - c. `doc_start`: documents are runs of positions, 6 of them; the first starts at 0 and the last at 3584; row r holds the start of the document of position pos[r].
All inputs are finite; a program needn't handle non-finite values.
Results may differ from the reference program's by a relative error of at most 0.0045.
Values may be sent and summed in bfloat16 or wider, within the bound.
No kernel may reach another device: no remote copies, remote signals or barrier semaphores. Data moves between devices by JAX's collectives and lax.ppermute only.
A program may use at most 192 MiB of HBM per device.

```python
import jax
import jax.numpy as jnp
from jax import lax

HEAD_DIM = 128
TOK_DEV = 256
NDOCS = 6
SPAN = 128
SPANS = 32
LENGTH = 4096
HEADS = 16
KV_HEADS = 1
N_CTX = 16


def layout_table(key):
    pair_count = SPANS // 2
    perm_key, flip_key = jax.random.split(jax.random.fold_in(key, 11))
    early = jax.random.permutation(perm_key, pair_count).astype(jnp.int32)
    flipped = jax.random.randint(flip_key, (pair_count,), 0, 2).astype(jnp.int32)
    late = SPANS - 1 - early
    leading = jnp.where(flipped == 1, late, early)
    trailing = jnp.where(flipped == 1, early, late)
    return jnp.stack([leading, trailing], axis=1).reshape(SPANS).astype(jnp.int32)


def draw_span_order(key, part):
    return layout_table(key)


def draw_doc_start(key, part):
    layout = layout_table(key)
    last_start = 7 * LENGTH // 8
    cut_points = jax.random.permutation(jax.random.fold_in(key, 12), last_start - 1)[:NDOCS - 2] + 1
    doc_firsts = jnp.concatenate([jnp.zeros((1,), jnp.int32), cut_points.astype(jnp.int32), jnp.full((1,), last_start, jnp.int32)])
    place_ids = jnp.arange(LENGTH, dtype=jnp.int32)
    first_pos = jnp.max(jnp.where(doc_firsts[None, :] <= place_ids[:, None], doc_firsts[None, :], 0), axis=1)
    row_ids = jnp.arange(LENGTH, dtype=jnp.int32)
    positions = layout[row_ids // SPAN] * SPAN + row_ids % SPAN
    return first_pos[positions].astype(jnp.int32)


def draw_key_base(key):
    drawn = jax.random.normal(jax.random.fold_in(key, 21), (LENGTH, KV_HEADS * HEAD_DIM), jnp.float32)
    drawn = jnp.clip(drawn, -6.0, 6.0) * 1.41
    return drawn


def draw_key_rows(key, part):
    return draw_key_base(key).astype(jnp.bfloat16)


def draw_queries(key, part):
    drawn = jax.random.normal(jax.random.fold_in(key, 22), (LENGTH, HEADS * HEAD_DIM), jnp.float32)
    drawn = jnp.clip(drawn, -6.0, 6.0) * 1.41
    return drawn.astype(jnp.bfloat16)


def levels(stream_key, shape, cuts, smallest, high):
    gain, own = 1.0, jax.random.fold_in(stream_key, 6)
    for dim, shards_of in cuts:
        draws = jnp.exp(jax.random.uniform(jax.random.fold_in(own, dim), (shards_of,), jnp.float32, smallest / len(cuts), high / len(cuts)))
        gain = gain * jnp.repeat(draws, shape[dim] // shards_of).reshape([-1 if axis == dim else 1 for axis in range(len(shape))])
    return gain


def bell_draw(own_key, shape, deviation, reach, pieces=(), kind=jnp.bfloat16):
    array = jax.random.normal(own_key, shape, jnp.float32) * deviation
    if len(pieces) > 0:
        array = levels(own_key, shape, pieces, -0.22, 0.18) * array
    return jnp.clip(array, min=-reach, max=reach).astype(kind)


def setup_inputs(seed: int = 0) -> dict:
    key_list = jax.random.split(jax.random.key(seed), 6)
    return {
        "queries": draw_queries(jax.random.fold_in(key_list[5], 71), 0),
        "key_rows": draw_key_rows(jax.random.fold_in(key_list[5], 71), 0),
        "value_rows": bell_draw(key_list[2], (LENGTH, KV_HEADS * HEAD_DIM), 1.0, 6.0, ((0, 32),)),
        "span_order": draw_span_order(jax.random.fold_in(key_list[5], 71), 0),
        "doc_start": draw_doc_start(jax.random.fold_in(key_list[5], 71), 0),
    }


NEG = -1.0e30


def reference(queries, key_rows, value_rows, span_order, doc_start):
    row_ids = jnp.arange(LENGTH, dtype=jnp.int32)
    positions = span_order[row_ids // SPAN].astype(jnp.int32) * SPAN + row_ids % SPAN
    group_size = HEADS // KV_HEADS
    score_scale = HEAD_DIM ** -0.5
    query_blocks = queries.reshape(N_CTX, TOK_DEV, KV_HEADS, group_size, HEAD_DIM)
    pos_blocks = positions.reshape(N_CTX, TOK_DEV)
    doc_blocks = doc_start.reshape(N_CTX, TOK_DEV)
    key_heads = key_rows.reshape(LENGTH, KV_HEADS, HEAD_DIM)
    value_heads = value_rows.reshape(LENGTH, KV_HEADS, HEAD_DIM)

    def per_group(kv_index):
        keys_here = key_heads[:, kv_index].astype(jnp.float32)
        values_here = value_heads[:, kv_index].astype(jnp.float32)

        def per_block(block_index):
            query_here = query_blocks[block_index][:, kv_index].astype(jnp.float32)
            pos_here = pos_blocks[block_index]
            doc_here = doc_blocks[block_index]
            visible = (doc_here[:, None] <= positions[None, :]) & (positions[None, :] <= pos_here[:, None])
            scores = jnp.einsum("qhd,kd->hqk", query_here, keys_here) * score_scale
            scores = jnp.where(visible[None], scores, NEG)
            row_max = jnp.max(scores, axis=2)
            weights = jnp.where(visible[None], jnp.exp(scores - row_max[:, :, None]), 0.0)
            totals = jnp.sum(weights, axis=2)
            rounded = lax.optimization_barrier(weights.astype(jnp.bfloat16)).astype(jnp.float32)
            mixed = jnp.einsum("hqk,kd->qhd", rounded, values_here)
            return (mixed / totals.T[:, :, None]).astype(jnp.bfloat16)

        return lax.map(per_block, jnp.arange(N_CTX, dtype=jnp.int32))

    outputs = lax.map(per_group, jnp.arange(KV_HEADS, dtype=jnp.int32))
    outputs = jnp.transpose(outputs, (1, 2, 0, 3, 4))
    return outputs.reshape(LENGTH, HEADS * HEAD_DIM)
```

```python
import functools

import jax
import jax.numpy as jnp
from jax import lax
from jax.experimental import pallas as pl
from jax.experimental.pallas import tpu as pltpu
from jax.sharding import PartitionSpec as P

HEAD_DIM = 128


NEG = -1e30


def attend_kernel(info_ref, inv_ref, q_ref, kv_ref, doc_ref, qpos_ref, o_ref,
                  qs_ref, m_ref, l_ref, acc_ref, *, heads, span_len, scale):
    j = pl.program_id(0)
    own = info_ref[0, j]
    low = info_ref[1, j]
    full_low = jnp.minimum(info_ref[2, j], own)
    rows = heads * span_len

    for h in range(heads):
        qs_ref[h * span_len:(h + 1) * span_len, :] = q_ref[:, h * HEAD_DIM:(h + 1) * HEAD_DIM]

    doc = doc_ref[...]
    qpos = qpos_ref[...]

    def block(p, masked, first):
        start = pl.multiple_of(inv_ref[p] * span_len, span_len)
        keys = kv_ref[pl.ds(start, span_len), 0:HEAD_DIM]
        vals = kv_ref[pl.ds(start, span_len), HEAD_DIM:2 * HEAD_DIM]
        scores = lax.dot_general(
            qs_ref[...], keys, (((1,), (1,)), ((), ())), preferred_element_type=jnp.float32
        )
        if masked:
            kpos = p * span_len + lax.broadcasted_iota(jnp.int32, (1, span_len), 1)
            visible = (kpos >= doc) & (kpos <= qpos)
            scores = jnp.where(
                visible[None], scores.reshape(heads, span_len, span_len), NEG
            ).reshape(rows, span_len)
        row_max = jnp.max(scores, axis=1, keepdims=True)
        if first:
            new_max = row_max
        else:
            old_max = m_ref[...]
            new_max = jnp.maximum(old_max, row_max)
            rescale = jnp.exp((old_max - new_max) * scale)
        weights = jnp.exp((scores - new_max) * scale)
        sums = jnp.sum(weights, axis=1, keepdims=True)
        mixed = jnp.dot(weights.astype(jnp.bfloat16), vals, preferred_element_type=jnp.float32)
        if first:
            l_ref[...] = sums
            acc_ref[...] = mixed
        else:
            l_ref[...] = rescale * l_ref[...] + sums
            acc_ref[...] = rescale * acc_ref[...] + mixed
        m_ref[...] = new_max

    block(own, True, True)

    def masked_step(p, carry):
        block(p, True, False)
        return carry

    def full_step(p, carry):
        block(p, False, False)
        return carry

    lax.fori_loop(low, full_low, masked_step, 0)
    lax.fori_loop(jnp.maximum(full_low, low), own, full_step, 0)

    out = acc_ref[...] / l_ref[...]
    for h in range(heads):
        o_ref[:, h * HEAD_DIM:(h + 1) * HEAD_DIM] = out[h * span_len:(h + 1) * span_len].astype(
            o_ref.dtype
        )


def on_device(queries, key_rows, value_rows, span_order, doc_start):
    tok_rows = queries.shape[0]
    heads = queries.shape[1] // HEAD_DIM
    kv_count = key_rows.shape[1] // HEAD_DIM
    n_ctx = lax.axis_size("ctx")
    n_head = lax.axis_size("head")
    ctx_index = lax.axis_index("ctx")
    n_spans = span_order.shape[0]
    length = key_rows.shape[0] * n_ctx * n_head
    span_len = length // n_spans
    n_local = tok_rows // span_len
    group_index = lax.axis_index("head") * kv_count // n_head

    if kv_count == 1:
        both = jnp.concatenate([key_rows, value_rows], axis=1)
        whole = lax.all_gather(both, ("ctx", "head"), axis=0, tiled=True)
    else:
        both = jnp.concatenate([key_rows, value_rows], axis=1)
        block_rows = lax.all_gather(both, "head", axis=0, tiled=True)
        own_keys = lax.dynamic_slice_in_dim(block_rows, group_index * HEAD_DIM, HEAD_DIM, 1)
        own_vals = lax.dynamic_slice_in_dim(
            block_rows, (kv_count + group_index) * HEAD_DIM, HEAD_DIM, 1
        )
        whole = lax.all_gather(
            jnp.concatenate([own_keys, own_vals], axis=1), "ctx", axis=0, tiled=True
        )

    slot_ids = jnp.arange(n_spans, dtype=jnp.int32)
    inverse = jnp.sum(
        jnp.where(span_order[None, :] == slot_ids[:, None], slot_ids[None, :], 0), axis=1
    ).astype(jnp.int32)
    local_slots = ctx_index * n_local + jnp.arange(n_local, dtype=jnp.int32)
    own_span = jnp.sum(
        jnp.where(local_slots[:, None] == slot_ids[None, :], span_order[None, :], 0), axis=1
    ).astype(jnp.int32)
    doc_spans = doc_start.reshape(n_local, span_len)
    low = jnp.min(doc_spans, axis=1) // span_len
    full_low = (jnp.max(doc_spans, axis=1) + span_len - 1) // span_len
    info = jnp.stack([own_span, low, full_low]).astype(jnp.int32)
    qpos = (own_span[:, None] * span_len + jnp.arange(span_len, dtype=jnp.int32)[None, :]).reshape(
        tok_rows, 1
    )
    doc_col = doc_start.reshape(tok_rows, 1)

    rows = heads * span_len
    kernel = functools.partial(
        attend_kernel, heads=heads, span_len=span_len, scale=HEAD_DIM ** (-0.5)
    )
    blocks_est = n_local * (n_spans // 2 + 1)
    cost = pl.CostEstimate(
        flops=4 * rows * span_len * HEAD_DIM * blocks_est,
        transcendentals=rows * span_len * blocks_est,
        bytes_accessed=2 * (queries.size * 2 + whole.size),
    )
    grid_spec = pltpu.PrefetchScalarGridSpec(
        num_scalar_prefetch=2,
        grid=(n_local,),
        in_specs=[
            pl.BlockSpec((span_len, heads * HEAD_DIM), lambda j, info, inv: (j, 0)),
            pl.BlockSpec((length, 2 * HEAD_DIM), lambda j, info, inv: (0, 0)),
            pl.BlockSpec((span_len, 1), lambda j, info, inv: (j, 0)),
            pl.BlockSpec((span_len, 1), lambda j, info, inv: (j, 0)),
        ],
        out_specs=pl.BlockSpec((span_len, heads * HEAD_DIM), lambda j, info, inv: (j, 0)),
        scratch_shapes=[
            pltpu.VMEM((rows, HEAD_DIM), jnp.bfloat16),
            pltpu.VMEM((rows, 1), jnp.float32),
            pltpu.VMEM((rows, 1), jnp.float32),
            pltpu.VMEM((rows, HEAD_DIM), jnp.float32),
        ],
    )
    return pl.pallas_call(
        kernel,
        grid_spec=grid_spec,
        out_shape=jax.ShapeDtypeStruct(queries.shape, queries.dtype),
        compiler_params=pltpu.CompilerParams(dimension_semantics=("arbitrary",)),
        cost_estimate=cost,
    )(info, inverse, queries, whole, doc_col, qpos)


def solution(mesh):
    in_specs = (P("ctx", "head"), P(("ctx", "head"), None), P(("ctx", "head"), None), P(), P("ctx"))
    out_specs = P("ctx", "head")
    return jax.shard_map(
        on_device, mesh=mesh, in_specs=in_specs, out_specs=out_specs, check_vma=False
    )
```

```python
import functools

import jax
import jax.numpy as jnp
from jax import lax
from jax.experimental import pallas as pl
from jax.experimental.pallas import tpu as pltpu
from jax.sharding import PartitionSpec as P

HEAD_DIM = 128


NEG = -1e30

ORDER_CORE0 = (4, 3, 2, 0)
ORDER_CORE1 = (0, 2, 4, 3)
CORE_BIT = 1


def doubling_gather(block, flat_index, n_dev):
    core = (flat_index >> CORE_BIT) & 1
    held = block
    for step in range(len(ORDER_CORE0)):
        pairs = []
        for k in range(n_dev):
            bit = ORDER_CORE0[step] if ((k >> CORE_BIT) & 1) == 0 else ORDER_CORE1[step]
            pairs.append((k, k ^ (1 << bit)))
        other = lax.ppermute(held, ("ctx", "head"), pairs)
        held = jnp.concatenate([held, other], axis=0)
    other = lax.ppermute(
        held, ("ctx", "head"), [(k, k ^ (1 << CORE_BIT)) for k in range(n_dev)]
    )
    held = jnp.concatenate([held, other], axis=0)

    def source_mask(order, j):
        mask = 0
        for t, bit in enumerate(order):
            mask = mask | (((j >> t) & 1) << bit)
        return mask

    half = 1 << len(ORDER_CORE0)
    j = jnp.arange(2 * half, dtype=jnp.int32)
    jl = j % half
    own_order_mask = jnp.where(core == 0, source_mask(ORDER_CORE0, jl), source_mask(ORDER_CORE1, jl))
    partner_order_mask = jnp.where(
        core == 0, source_mask(ORDER_CORE1, jl), source_mask(ORDER_CORE0, jl)
    )
    partner = flat_index ^ (1 << CORE_BIT)
    source = jnp.where(j < half, flat_index ^ own_order_mask, partner ^ partner_order_mask)
    return held, source


def attend_kernel(info_ref, slot_ref, qt_ref, kv_ref, doc_ref, qpos_ref, o_ref,
                  m_ref, l_ref, acc_ref, *, heads, span_len, scale):
    j = pl.program_id(0)
    own = info_ref[0, j]
    low = info_ref[1, j]
    full_low = jnp.minimum(info_ref[2, j], own)

    doc = doc_ref[...]
    qpos = qpos_ref[...]

    def block(p, masked, first):
        b = slot_ref[p]
        keys = kv_ref[b, 0]
        vals_t = kv_ref[b, 1]
        scores = jnp.dot(keys, qt_ref[...], preferred_element_type=jnp.float32)
        if masked:
            kpos = p * span_len + lax.broadcasted_iota(jnp.int32, (span_len, 1), 0)
            visible = (kpos >= doc) & (kpos <= qpos)
            scores = jnp.where(visible, scores, NEG)
        col_max = jnp.max(scores, axis=0, keepdims=True)
        if first:
            new_max = col_max
        else:
            old_max = m_ref[...]
            new_max = jnp.maximum(old_max, col_max)
            rescale = jnp.exp((old_max - new_max) * scale)
        weights = jnp.exp((scores - new_max) * scale)
        sums = jnp.sum(weights, axis=0, keepdims=True)
        mixed = jnp.dot(vals_t, weights.astype(jnp.bfloat16), preferred_element_type=jnp.float32)
        if first:
            l_ref[...] = sums
            acc_ref[...] = mixed
        else:
            l_ref[...] = rescale * l_ref[...] + sums
            acc_ref[...] = rescale * acc_ref[...] + mixed
        m_ref[...] = new_max

    block(own, True, True)

    def masked_step(p, carry):
        block(p, True, False)
        return carry

    def full_step(p, carry):
        block(p, False, False)
        return carry

    lax.fori_loop(low, full_low, masked_step, 0)
    lax.fori_loop(jnp.maximum(full_low, low), own, full_step, 0)

    out_t = acc_ref[...] / l_ref[...]
    for h in range(heads):
        o_ref[:, h * HEAD_DIM:(h + 1) * HEAD_DIM] = out_t[:, h * span_len:(h + 1) * span_len].T.astype(
            o_ref.dtype
        )


def span_blocks(rows, span_len):
    n = rows.shape[0] // span_len
    keys = rows[:, :HEAD_DIM].reshape(n, span_len, HEAD_DIM)
    vals_t = jnp.swapaxes(rows[:, HEAD_DIM:].reshape(n, span_len, HEAD_DIM), 1, 2)
    return jnp.stack([keys, vals_t], axis=1)


def on_device(queries, key_rows, value_rows, span_order, doc_start):
    tok_rows = queries.shape[0]
    heads = queries.shape[1] // HEAD_DIM
    kv_count = key_rows.shape[1] // HEAD_DIM
    n_ctx = lax.axis_size("ctx")
    n_head = lax.axis_size("head")
    n_dev = n_ctx * n_head
    ctx_index = lax.axis_index("ctx")
    n_spans = span_order.shape[0]
    length = key_rows.shape[0] * n_dev
    span_len = length // n_spans
    n_local = tok_rows // span_len
    group_index = lax.axis_index("head") * kv_count // n_head
    slot_ids = jnp.arange(n_spans, dtype=jnp.int32)

    if kv_count == 1 and n_dev == 32 and key_rows.shape[0] == span_len:
        flat_index = ctx_index * n_head + lax.axis_index("head")
        local = span_blocks(jnp.concatenate([key_rows, value_rows], axis=1), span_len)
        whole, source = doubling_gather(local, flat_index, n_dev)
    else:
        both = jnp.concatenate([key_rows, value_rows], axis=1)
        block_rows = lax.all_gather(both, "head", axis=0, tiled=True)
        own_keys = lax.dynamic_slice_in_dim(block_rows, group_index * HEAD_DIM, HEAD_DIM, 1)
        own_vals = lax.dynamic_slice_in_dim(
            block_rows, (kv_count + group_index) * HEAD_DIM, HEAD_DIM, 1
        )
        local = span_blocks(jnp.concatenate([own_keys, own_vals], axis=1), span_len)
        whole = lax.all_gather(local, "ctx", axis=0, tiled=True)
        source = slot_ids

    inverse = jnp.sum(
        jnp.where(span_order[None, :] == slot_ids[:, None], slot_ids[None, :], 0), axis=1
    ).astype(jnp.int32)
    where_held = jnp.sum(
        jnp.where(inverse[:, None] == source[None, :], slot_ids[None, :], 0), axis=1
    ).astype(jnp.int32)

    local_slots = ctx_index * n_local + jnp.arange(n_local, dtype=jnp.int32)
    own_span = jnp.sum(
        jnp.where(local_slots[:, None] == slot_ids[None, :], span_order[None, :], 0), axis=1
    ).astype(jnp.int32)
    doc_spans = doc_start.reshape(n_local, span_len)
    low = jnp.min(doc_spans, axis=1) // span_len
    full_low = (jnp.max(doc_spans, axis=1) + span_len - 1) // span_len
    info = jnp.stack([own_span, low, full_low]).astype(jnp.int32)

    rows = heads * span_len
    qpos = own_span[:, None] * span_len + jnp.arange(span_len, dtype=jnp.int32)[None, :]
    qpos_cols = jnp.broadcast_to(qpos[:, None, None, :], (n_local, 1, heads, span_len)).reshape(
        n_local, 1, rows
    )
    doc_cols = jnp.broadcast_to(
        doc_spans[:, None, None, :], (n_local, 1, heads, span_len)
    ).reshape(n_local, 1, rows)
    q_t = jnp.transpose(
        queries.reshape(n_local, span_len, heads, HEAD_DIM), (0, 3, 2, 1)
    ).reshape(n_local, HEAD_DIM, rows)

    kernel = functools.partial(
        attend_kernel, heads=heads, span_len=span_len, scale=HEAD_DIM ** (-0.5)
    )
    blocks_est = n_local * (n_spans // 2 + 1)
    cost = pl.CostEstimate(
        flops=4 * rows * span_len * HEAD_DIM * blocks_est,
        transcendentals=rows * span_len * blocks_est,
        bytes_accessed=2 * (queries.size * 2 + whole.size),
    )
    grid_spec = pltpu.PrefetchScalarGridSpec(
        num_scalar_prefetch=2,
        grid=(n_local,),
        in_specs=[
            pl.BlockSpec((None, HEAD_DIM, rows), lambda j, info, slot: (j, 0, 0)),
            pl.BlockSpec(whole.shape, lambda j, info, slot: (0, 0, 0, 0)),
            pl.BlockSpec((None, 1, rows), lambda j, info, slot: (j, 0, 0)),
            pl.BlockSpec((None, 1, rows), lambda j, info, slot: (j, 0, 0)),
        ],
        out_specs=pl.BlockSpec((span_len, heads * HEAD_DIM), lambda j, info, slot: (j, 0)),
        scratch_shapes=[
            pltpu.VMEM((1, rows), jnp.float32),
            pltpu.VMEM((1, rows), jnp.float32),
            pltpu.VMEM((HEAD_DIM, rows), jnp.float32),
        ],
    )
    return pl.pallas_call(
        kernel,
        grid_spec=grid_spec,
        out_shape=jax.ShapeDtypeStruct(queries.shape, queries.dtype),
        compiler_params=pltpu.CompilerParams(dimension_semantics=("arbitrary",)),
        cost_estimate=cost,
    )(info, where_held, q_t, whole, doc_cols, qpos_cols)


def solution(mesh):
    in_specs = (P("ctx", "head"), P(("ctx", "head"), None), P(("ctx", "head"), None), P(), P("ctx"))
    out_specs = P("ctx", "head")
    return jax.shard_map(
        on_device, mesh=mesh, in_specs=in_specs, out_specs=out_specs, check_vma=False
    )
```

```python
import functools

import jax
import jax.numpy as jnp
from jax import lax
from jax.experimental import pallas as pl
from jax.experimental.pallas import tpu as pltpu
from jax.sharding import PartitionSpec as P

HEAD_DIM = 128


NEG = -1e30

ORDER_CORE0 = (4, 3, 2, 0)
ORDER_CORE1 = (0, 2, 4, 3)
CORE_BIT = 1


def doubling_gather(block, flat_index, n_dev):
    core = (flat_index >> CORE_BIT) & 1
    held = block
    for step in range(len(ORDER_CORE0)):
        pairs = []
        for k in range(n_dev):
            bit = ORDER_CORE0[step] if ((k >> CORE_BIT) & 1) == 0 else ORDER_CORE1[step]
            pairs.append((k, k ^ (1 << bit)))
        other = lax.ppermute(held, ("ctx", "head"), pairs)
        held = jnp.concatenate([held, other], axis=0)
    other = lax.ppermute(
        held, ("ctx", "head"), [(k, k ^ (1 << CORE_BIT)) for k in range(n_dev)]
    )

    def source_mask(order, j):
        mask = 0
        for t, bit in enumerate(order):
            mask = mask | (((j >> t) & 1) << bit)
        return mask

    half = 1 << len(ORDER_CORE0)
    j = jnp.arange(2 * half, dtype=jnp.int32)
    jl = j % half
    own_order_mask = jnp.where(core == 0, source_mask(ORDER_CORE0, jl), source_mask(ORDER_CORE1, jl))
    partner_order_mask = jnp.where(
        core == 0, source_mask(ORDER_CORE1, jl), source_mask(ORDER_CORE0, jl)
    )
    partner = flat_index ^ (1 << CORE_BIT)
    source = jnp.where(j < half, flat_index ^ own_order_mask, partner ^ partner_order_mask)
    return held, other, source


def attend_kernel(info_ref, slot_ref, qt_ref, first_ref, second_ref, doc_ref, o_ref,
                  m_ref, l_ref, acc_ref, *, heads, span_len, scale):
    j = pl.program_id(0)
    own = info_ref[0, j]
    low = info_ref[1, j]
    full_low = jnp.minimum(info_ref[2, j], own)
    half = first_ref.shape[0]
    rows = heads * span_len

    doc_row = doc_ref[...]
    doc = jnp.concatenate([doc_row] * heads, axis=1)
    cols = lax.broadcasted_iota(jnp.int32, (1, rows), 1)
    qpos = own * span_len + lax.rem(cols, span_len)

    def block(p, masked, first):
        b = slot_ref[p]
        in_first = b < half
        bl = lax.rem(b, half)
        kv = jnp.where(in_first, first_ref[bl], second_ref[bl])
        keys = kv[:, :HEAD_DIM]
        vals_t = kv[:, HEAD_DIM:].T
        scores = jnp.dot(keys, qt_ref[...], preferred_element_type=jnp.float32)
        if masked:
            kpos = p * span_len + lax.broadcasted_iota(jnp.int32, (span_len, 1), 0)
            visible = (kpos >= doc) & (kpos <= qpos)
            scores = jnp.where(visible, scores, NEG)
        col_max = jnp.max(scores, axis=0, keepdims=True)
        if first:
            new_max = col_max
        else:
            old_max = m_ref[...]
            new_max = jnp.maximum(old_max, col_max)
            rescale = jnp.exp((old_max - new_max) * scale)
        weights = jnp.exp((scores - new_max) * scale)
        sums = jnp.sum(weights, axis=0, keepdims=True)
        mixed = jnp.dot(vals_t, weights.astype(jnp.bfloat16), preferred_element_type=jnp.float32)
        if first:
            l_ref[...] = sums
            acc_ref[...] = mixed
        else:
            l_ref[...] = rescale * l_ref[...] + sums
            acc_ref[...] = rescale * acc_ref[...] + mixed
        m_ref[...] = new_max

    block(own, True, True)

    def masked_step(p, carry):
        block(p, True, False)
        return carry

    def full_step(p, carry):
        block(p, False, False)
        return carry

    lax.fori_loop(low, full_low, masked_step, 0)
    lax.fori_loop(jnp.maximum(full_low, low), own, full_step, 0)

    out_t = acc_ref[...] / l_ref[...]
    for h in range(heads):
        o_ref[:, h * HEAD_DIM:(h + 1) * HEAD_DIM] = out_t[:, h * span_len:(h + 1) * span_len].T.astype(
            o_ref.dtype
        )


def span_blocks(rows, span_len):
    return rows.reshape(rows.shape[0] // span_len, span_len, 2 * HEAD_DIM)


def on_device(queries, key_rows, value_rows, span_order, doc_start):
    tok_rows = queries.shape[0]
    heads = queries.shape[1] // HEAD_DIM
    kv_count = key_rows.shape[1] // HEAD_DIM
    n_ctx = lax.axis_size("ctx")
    n_head = lax.axis_size("head")
    n_dev = n_ctx * n_head
    ctx_index = lax.axis_index("ctx")
    n_spans = span_order.shape[0]
    length = key_rows.shape[0] * n_dev
    span_len = length // n_spans
    n_local = tok_rows // span_len
    group_index = lax.axis_index("head") * kv_count // n_head
    slot_ids = jnp.arange(n_spans, dtype=jnp.int32)

    if kv_count == 1 and n_dev == 32 and key_rows.shape[0] == span_len:
        flat_index = ctx_index * n_head + lax.axis_index("head")
        local = span_blocks(jnp.concatenate([key_rows, value_rows], axis=1), span_len)
        first_half, second_half, source = doubling_gather(local, flat_index, n_dev)
    else:
        both = jnp.concatenate([key_rows, value_rows], axis=1)
        block_rows = lax.all_gather(both, "head", axis=0, tiled=True)
        own_keys = lax.dynamic_slice_in_dim(block_rows, group_index * HEAD_DIM, HEAD_DIM, 1)
        own_vals = lax.dynamic_slice_in_dim(
            block_rows, (kv_count + group_index) * HEAD_DIM, HEAD_DIM, 1
        )
        local = span_blocks(jnp.concatenate([own_keys, own_vals], axis=1), span_len)
        whole = lax.all_gather(local, "ctx", axis=0, tiled=True)
        first_half, second_half = whole[: n_spans // 2], whole[n_spans // 2:]
        source = slot_ids

    inverse = jnp.sum(
        jnp.where(span_order[None, :] == slot_ids[:, None], slot_ids[None, :], 0), axis=1
    ).astype(jnp.int32)
    where_held = jnp.sum(
        jnp.where(inverse[:, None] == source[None, :], slot_ids[None, :], 0), axis=1
    ).astype(jnp.int32)

    local_slots = ctx_index * n_local + jnp.arange(n_local, dtype=jnp.int32)
    own_span = jnp.sum(
        jnp.where(local_slots[:, None] == slot_ids[None, :], span_order[None, :], 0), axis=1
    ).astype(jnp.int32)
    doc_spans = doc_start.reshape(n_local, span_len)
    low = jnp.min(doc_spans, axis=1) // span_len
    full_low = (jnp.max(doc_spans, axis=1) + span_len - 1) // span_len
    info = jnp.stack([own_span, low, full_low]).astype(jnp.int32)

    rows = heads * span_len
    doc_rows = doc_start.reshape(n_local, 1, span_len)
    q_t = jnp.transpose(
        queries.reshape(n_local, span_len, heads, HEAD_DIM), (0, 3, 2, 1)
    ).reshape(n_local, HEAD_DIM, rows)

    kernel = functools.partial(
        attend_kernel, heads=heads, span_len=span_len, scale=HEAD_DIM ** (-0.5)
    )
    blocks_est = n_local * (n_spans // 2 + 1)
    cost = pl.CostEstimate(
        flops=4 * rows * span_len * HEAD_DIM * blocks_est,
        transcendentals=rows * span_len * blocks_est,
        bytes_accessed=2 * (queries.size * 2 + first_half.size + second_half.size),
    )
    grid_spec = pltpu.PrefetchScalarGridSpec(
        num_scalar_prefetch=2,
        grid=(n_local,),
        in_specs=[
            pl.BlockSpec((None, HEAD_DIM, rows), lambda j, info, slot: (j, 0, 0)),
            pl.BlockSpec(first_half.shape, lambda j, info, slot: (0, 0, 0)),
            pl.BlockSpec(second_half.shape, lambda j, info, slot: (0, 0, 0)),
            pl.BlockSpec((None, 1, span_len), lambda j, info, slot: (j, 0, 0)),
        ],
        out_specs=pl.BlockSpec((span_len, heads * HEAD_DIM), lambda j, info, slot: (j, 0)),
        scratch_shapes=[
            pltpu.VMEM((1, rows), jnp.float32),
            pltpu.VMEM((1, rows), jnp.float32),
            pltpu.VMEM((HEAD_DIM, rows), jnp.float32),
        ],
    )
    return pl.pallas_call(
        kernel,
        grid_spec=grid_spec,
        out_shape=jax.ShapeDtypeStruct(queries.shape, queries.dtype),
        compiler_params=pltpu.CompilerParams(dimension_semantics=("arbitrary",)),
        cost_estimate=cost,
    )(info, where_held, q_t, first_half, second_half, doc_rows)


def solution(mesh):
    in_specs = (P("ctx", "head"), P(("ctx", "head"), None), P(("ctx", "head"), None), P(), P("ctx"))
    out_specs = P("ctx", "head")
    return jax.shard_map(
        on_device, mesh=mesh, in_specs=in_specs, out_specs=out_specs, check_vma=False
    )
```

```python
import functools

import jax
import jax.numpy as jnp
from jax import lax
from jax.experimental import pallas as pl
from jax.experimental.pallas import tpu as pltpu
from jax.sharding import PartitionSpec as P

HEAD_DIM = 128


NEG = -1e30

ORDER_CORE0 = (4, 3, 2, 0)
ORDER_CORE1 = (0, 2, 4, 3)
CORE_BIT = 1


def doubling_gather(block, flat_index, n_dev):
    core = (flat_index >> CORE_BIT) & 1
    held = block
    for step in range(len(ORDER_CORE0)):
        pairs = []
        for k in range(n_dev):
            bit = ORDER_CORE0[step] if ((k >> CORE_BIT) & 1) == 0 else ORDER_CORE1[step]
            pairs.append((k, k ^ (1 << bit)))
        other = lax.ppermute(held, ("ctx", "head"), pairs)
        held = jnp.concatenate([held, other], axis=0)
    other = lax.ppermute(
        held, ("ctx", "head"), [(k, k ^ (1 << CORE_BIT)) for k in range(n_dev)]
    )

    def source_mask(order, j):
        mask = 0
        for t, bit in enumerate(order):
            mask = mask | (((j >> t) & 1) << bit)
        return mask

    half = 1 << len(ORDER_CORE0)
    j = jnp.arange(2 * half, dtype=jnp.int32)
    jl = j % half
    own_order_mask = jnp.where(core == 0, source_mask(ORDER_CORE0, jl), source_mask(ORDER_CORE1, jl))
    partner_order_mask = jnp.where(
        core == 0, source_mask(ORDER_CORE1, jl), source_mask(ORDER_CORE0, jl)
    )
    partner = flat_index ^ (1 << CORE_BIT)
    source = jnp.where(j < half, flat_index ^ own_order_mask, partner ^ partner_order_mask)
    return held, other, source


def attend_kernel(info_ref, slot_ref, qt_ref, first_ref, second_ref, doc_ref, o_ref,
                  m_ref, l_ref, acc_ref, *, heads, span_len, scale):
    j = pl.program_id(0)
    own = info_ref[0, j]
    low = info_ref[1, j]
    full_low = jnp.minimum(info_ref[2, j], own)
    half = first_ref.shape[0]
    rows = heads * span_len

    doc_row = doc_ref[...]
    doc = jnp.concatenate([doc_row] * heads, axis=1)
    cols = lax.broadcasted_iota(jnp.int32, (1, rows), 1)
    qpos = own * span_len + lax.rem(cols, span_len)

    def block(p, masked, first):
        b = slot_ref[p]
        in_first = b < half
        bl = lax.rem(b, half)
        kv = jnp.where(in_first, first_ref[bl], second_ref[bl])
        keys = kv[:, :HEAD_DIM]
        vals_t = kv[:, HEAD_DIM:]
        scores = jnp.dot(keys, qt_ref[...], preferred_element_type=jnp.float32)
        if masked:
            kpos = p * span_len + lax.broadcasted_iota(jnp.int32, (span_len, 1), 0)
            visible = (kpos >= doc) & (kpos <= qpos)
            scores = jnp.where(visible, scores, NEG)
        col_max = jnp.max(scores, axis=0, keepdims=True)
        if first:
            new_max = col_max
        else:
            old_max = m_ref[...]
            new_max = jnp.maximum(old_max, col_max)
            rescale = jnp.exp((old_max - new_max) * scale)
        weights = jnp.exp((scores - new_max) * scale)
        sums = jnp.sum(weights, axis=0, keepdims=True)
        mixed = jnp.dot(vals_t, weights.astype(jnp.bfloat16), preferred_element_type=jnp.float32)
        if first:
            l_ref[...] = sums
            acc_ref[...] = mixed
        else:
            l_ref[...] = rescale * l_ref[...] + sums
            acc_ref[...] = rescale * acc_ref[...] + mixed
        m_ref[...] = new_max

    block(own, True, True)

    def masked_step(p, carry):
        block(p, True, False)
        return carry

    def full_step(p, carry):
        block(p, False, False)
        return carry

    lax.fori_loop(low, full_low, masked_step, 0)
    lax.fori_loop(jnp.maximum(full_low, low), own, full_step, 0)

    out_t = acc_ref[...] / l_ref[...]
    for h in range(heads):
        o_ref[:, h * HEAD_DIM:(h + 1) * HEAD_DIM] = out_t[:, h * span_len:(h + 1) * span_len].T.astype(
            o_ref.dtype
        )


def span_blocks(keys, vals, span_len):
    n = keys.shape[0] // span_len
    vals_t = jnp.swapaxes(vals.reshape(n, span_len, HEAD_DIM), 1, 2)
    return jnp.concatenate([keys.reshape(n, span_len, HEAD_DIM), vals_t], axis=2)


def on_device(queries, key_rows, value_rows, span_order, doc_start):
    tok_rows = queries.shape[0]
    heads = queries.shape[1] // HEAD_DIM
    kv_count = key_rows.shape[1] // HEAD_DIM
    n_ctx = lax.axis_size("ctx")
    n_head = lax.axis_size("head")
    n_dev = n_ctx * n_head
    ctx_index = lax.axis_index("ctx")
    n_spans = span_order.shape[0]
    length = key_rows.shape[0] * n_dev
    span_len = length // n_spans
    n_local = tok_rows // span_len
    group_index = lax.axis_index("head") * kv_count // n_head
    slot_ids = jnp.arange(n_spans, dtype=jnp.int32)

    if kv_count == 1 and n_dev == 32 and key_rows.shape[0] == span_len:
        flat_index = ctx_index * n_head + lax.axis_index("head")
        local = span_blocks(key_rows, value_rows, span_len)
        first_half, second_half, source = doubling_gather(local, flat_index, n_dev)
    else:
        both = jnp.concatenate([key_rows, value_rows], axis=1)
        block_rows = lax.all_gather(both, "head", axis=0, tiled=True)
        own_keys = lax.dynamic_slice_in_dim(block_rows, group_index * HEAD_DIM, HEAD_DIM, 1)
        own_vals = lax.dynamic_slice_in_dim(
            block_rows, (kv_count + group_index) * HEAD_DIM, HEAD_DIM, 1
        )
        local = span_blocks(own_keys, own_vals, span_len)
        whole = lax.all_gather(local, "ctx", axis=0, tiled=True)
        first_half, second_half = whole[: n_spans // 2], whole[n_spans // 2:]
        source = slot_ids

    inverse = jnp.sum(
        jnp.where(span_order[None, :] == slot_ids[:, None], slot_ids[None, :], 0), axis=1
    ).astype(jnp.int32)
    where_held = jnp.sum(
        jnp.where(inverse[:, None] == source[None, :], slot_ids[None, :], 0), axis=1
    ).astype(jnp.int32)

    local_slots = ctx_index * n_local + jnp.arange(n_local, dtype=jnp.int32)
    own_span = jnp.sum(
        jnp.where(local_slots[:, None] == slot_ids[None, :], span_order[None, :], 0), axis=1
    ).astype(jnp.int32)
    doc_spans = doc_start.reshape(n_local, span_len)
    low = jnp.min(doc_spans, axis=1) // span_len
    full_low = (jnp.max(doc_spans, axis=1) + span_len - 1) // span_len
    info = jnp.stack([own_span, low, full_low]).astype(jnp.int32)

    rows = heads * span_len
    doc_rows = doc_start.reshape(n_local, 1, span_len)
    q_t = jnp.transpose(
        queries.reshape(n_local, span_len, heads, HEAD_DIM), (0, 3, 2, 1)
    ).reshape(n_local, HEAD_DIM, rows)

    kernel = functools.partial(
        attend_kernel, heads=heads, span_len=span_len, scale=HEAD_DIM ** (-0.5)
    )
    blocks_est = n_local * (n_spans // 2 + 1)
    cost = pl.CostEstimate(
        flops=4 * rows * span_len * HEAD_DIM * blocks_est,
        transcendentals=rows * span_len * blocks_est,
        bytes_accessed=2 * (queries.size * 2 + first_half.size + second_half.size),
    )
    grid_spec = pltpu.PrefetchScalarGridSpec(
        num_scalar_prefetch=2,
        grid=(n_local,),
        in_specs=[
            pl.BlockSpec((None, HEAD_DIM, rows), lambda j, info, slot: (j, 0, 0)),
            pl.BlockSpec(first_half.shape, lambda j, info, slot: (0, 0, 0)),
            pl.BlockSpec(second_half.shape, lambda j, info, slot: (0, 0, 0)),
            pl.BlockSpec((None, 1, span_len), lambda j, info, slot: (j, 0, 0)),
        ],
        out_specs=pl.BlockSpec((span_len, heads * HEAD_DIM), lambda j, info, slot: (j, 0)),
        scratch_shapes=[
            pltpu.VMEM((1, rows), jnp.float32),
            pltpu.VMEM((1, rows), jnp.float32),
            pltpu.VMEM((HEAD_DIM, rows), jnp.float32),
        ],
    )
    return pl.pallas_call(
        kernel,
        grid_spec=grid_spec,
        out_shape=jax.ShapeDtypeStruct(queries.shape, queries.dtype),
        compiler_params=pltpu.CompilerParams(dimension_semantics=("arbitrary",)),
        cost_estimate=cost,
    )(info, where_held, q_t, first_half, second_half, doc_rows)


def solution(mesh):
    in_specs = (P("ctx", "head"), P(("ctx", "head"), None), P(("ctx", "head"), None), P(), P("ctx"))
    out_specs = P("ctx", "head")
    return jax.shard_map(
        on_device, mesh=mesh, in_specs=in_specs, out_specs=out_specs, check_vma=False
    )
```

```python
import functools

import jax
import jax.numpy as jnp
from jax import lax
from jax.experimental import pallas as pl
from jax.experimental.pallas import tpu as pltpu
from jax.sharding import PartitionSpec as P

HEAD_DIM = 128


NEG = -1e30

ORDER_CORE0 = (4, 3, 2, 0)
ORDER_CORE1 = (0, 2, 4, 3)
CORE_BIT = 1


def doubling_gather(block, flat_index, n_dev):
    core = (flat_index >> CORE_BIT) & 1
    held = block
    pieces = []
    for step in range(len(ORDER_CORE0)):
        pairs = []
        for k in range(n_dev):
            bit = ORDER_CORE0[step] if ((k >> CORE_BIT) & 1) == 0 else ORDER_CORE1[step]
            pairs.append((k, k ^ (1 << bit)))
        other = lax.ppermute(held, ("ctx", "head"), pairs)
        if step == len(ORDER_CORE0) - 1:
            pieces.append(held)
            pieces.append(other)
        held = jnp.concatenate([held, other], axis=0)
    other = lax.ppermute(
        held, ("ctx", "head"), [(k, k ^ (1 << CORE_BIT)) for k in range(n_dev)]
    )
    pieces.append(other)

    def source_mask(order, j):
        mask = 0
        for t, bit in enumerate(order):
            mask = mask | (((j >> t) & 1) << bit)
        return mask

    half = 1 << len(ORDER_CORE0)
    j = jnp.arange(2 * half, dtype=jnp.int32)
    jl = j % half
    own_order_mask = jnp.where(core == 0, source_mask(ORDER_CORE0, jl), source_mask(ORDER_CORE1, jl))
    partner_order_mask = jnp.where(
        core == 0, source_mask(ORDER_CORE1, jl), source_mask(ORDER_CORE0, jl)
    )
    partner = flat_index ^ (1 << CORE_BIT)
    source = jnp.where(j < half, flat_index ^ own_order_mask, partner ^ partner_order_mask)
    return pieces, source


def attend_kernel(info_ref, slot_ref, qt_ref, kv_ref, doc_ref, *rest,
                  heads, span_len, scale, base, first, last):
    rest = list(rest)
    if not first:
        im_ref, il_ref, iacc_ref = rest[:3]
        rest = rest[3:]
    if last:
        o_ref = rest[0]
        rest = rest[1:]
    else:
        om_ref, ol_ref, oacc_ref = rest[:3]
        rest = rest[3:]
    m_ref, l_ref, acc_ref = rest
    j = pl.program_id(0)
    own = info_ref[0, j]
    low = info_ref[1, j]
    full_low = jnp.minimum(info_ref[2, j], own)
    count = kv_ref.shape[0]
    rows = heads * span_len

    if first:
        m_ref[...] = jnp.full(m_ref.shape, NEG, jnp.float32)
        l_ref[...] = jnp.zeros(l_ref.shape, jnp.float32)
        acc_ref[...] = jnp.zeros(acc_ref.shape, jnp.float32)
    else:
        m_ref[...] = im_ref[...]
        l_ref[...] = il_ref[...]
        acc_ref[...] = iacc_ref[...]

    doc_row = doc_ref[...]
    doc = jnp.concatenate([doc_row] * heads, axis=1)
    cols = lax.broadcasted_iota(jnp.int32, (1, rows), 1)
    qpos = own * span_len + lax.rem(cols, span_len)

    def block(p, masked):
        b = slot_ref[p] - base

        @pl.when((b >= 0) & (b < count))
        def _():
            kv = kv_ref[b]
            keys = kv[:, :HEAD_DIM]
            vals_t = kv[:, HEAD_DIM:]
            scores = jnp.dot(keys, qt_ref[...], preferred_element_type=jnp.float32)
            if masked:
                kpos = p * span_len + lax.broadcasted_iota(jnp.int32, (span_len, 1), 0)
                visible = (kpos >= doc) & (kpos <= qpos)
                scores = jnp.where(visible, scores, NEG)
            old_max = m_ref[...]
            new_max = jnp.maximum(old_max, jnp.max(scores, axis=0, keepdims=True))
            rescale = jnp.exp((old_max - new_max) * scale)
            weights = jnp.exp((scores - new_max) * scale)
            if masked:
                weights = jnp.where(visible, weights, 0.0)
            sums = jnp.sum(weights, axis=0, keepdims=True)
            mixed = jnp.dot(vals_t, weights.astype(jnp.bfloat16), preferred_element_type=jnp.float32)
            l_ref[...] = rescale * l_ref[...] + sums
            acc_ref[...] = rescale * acc_ref[...] + mixed
            m_ref[...] = new_max

    block(own, True)

    def masked_step(p, carry):
        block(p, True)
        return carry

    def full_step(p, carry):
        block(p, False)
        return carry

    lax.fori_loop(low, full_low, masked_step, 0)
    lax.fori_loop(jnp.maximum(full_low, low), own, full_step, 0)

    if last:
        out_t = acc_ref[...] / l_ref[...]
        for h in range(heads):
            o_ref[:, h * HEAD_DIM:(h + 1) * HEAD_DIM] = out_t[
                :, h * span_len:(h + 1) * span_len
            ].T.astype(o_ref.dtype)
    else:
        om_ref[...] = m_ref[...]
        ol_ref[...] = l_ref[...]
        oacc_ref[...] = acc_ref[...]


def span_blocks(keys, vals, span_len):
    n = keys.shape[0] // span_len
    vals_t = jnp.swapaxes(vals.reshape(n, span_len, HEAD_DIM), 1, 2)
    return jnp.concatenate([keys.reshape(n, span_len, HEAD_DIM), vals_t], axis=2)


def on_device(queries, key_rows, value_rows, span_order, doc_start):
    tok_rows = queries.shape[0]
    heads = queries.shape[1] // HEAD_DIM
    kv_count = key_rows.shape[1] // HEAD_DIM
    n_ctx = lax.axis_size("ctx")
    n_head = lax.axis_size("head")
    n_dev = n_ctx * n_head
    ctx_index = lax.axis_index("ctx")
    n_spans = span_order.shape[0]
    length = key_rows.shape[0] * n_dev
    span_len = length // n_spans
    n_local = tok_rows // span_len
    group_index = lax.axis_index("head") * kv_count // n_head
    slot_ids = jnp.arange(n_spans, dtype=jnp.int32)

    if kv_count == 1 and n_dev == 32 and key_rows.shape[0] == span_len:
        flat_index = ctx_index * n_head + lax.axis_index("head")
        local = span_blocks(key_rows, value_rows, span_len)
        pieces, source = doubling_gather(local, flat_index, n_dev)
    else:
        both = jnp.concatenate([key_rows, value_rows], axis=1)
        block_rows = lax.all_gather(both, "head", axis=0, tiled=True)
        own_keys = lax.dynamic_slice_in_dim(block_rows, group_index * HEAD_DIM, HEAD_DIM, 1)
        own_vals = lax.dynamic_slice_in_dim(
            block_rows, (kv_count + group_index) * HEAD_DIM, HEAD_DIM, 1
        )
        local = span_blocks(own_keys, own_vals, span_len)
        whole = lax.all_gather(local, "ctx", axis=0, tiled=True)
        pieces = [whole]
        source = slot_ids

    inverse = jnp.sum(
        jnp.where(span_order[None, :] == slot_ids[:, None], slot_ids[None, :], 0), axis=1
    ).astype(jnp.int32)
    where_held = jnp.sum(
        jnp.where(inverse[:, None] == source[None, :], slot_ids[None, :], 0), axis=1
    ).astype(jnp.int32)

    local_slots = ctx_index * n_local + jnp.arange(n_local, dtype=jnp.int32)
    own_span = jnp.sum(
        jnp.where(local_slots[:, None] == slot_ids[None, :], span_order[None, :], 0), axis=1
    ).astype(jnp.int32)
    doc_spans = doc_start.reshape(n_local, span_len)
    low = jnp.min(doc_spans, axis=1) // span_len
    full_low = (jnp.max(doc_spans, axis=1) + span_len - 1) // span_len
    info = jnp.stack([own_span, low, full_low]).astype(jnp.int32)

    rows = heads * span_len
    doc_rows = doc_start.reshape(n_local, 1, span_len)
    q_t = jnp.transpose(
        queries.reshape(n_local, span_len, heads, HEAD_DIM), (0, 3, 2, 1)
    ).reshape(n_local, HEAD_DIM, rows)

    blocks_est = n_local * (n_spans // 2 + 1)
    state_shapes = [
        jax.ShapeDtypeStruct((n_local, 1, rows), jnp.float32),
        jax.ShapeDtypeStruct((n_local, 1, rows), jnp.float32),
        jax.ShapeDtypeStruct((n_local, HEAD_DIM, rows), jnp.float32),
    ]
    state_specs = [
        pl.BlockSpec((None, 1, rows), lambda j, info, slot: (j, 0, 0)),
        pl.BlockSpec((None, 1, rows), lambda j, info, slot: (j, 0, 0)),
        pl.BlockSpec((None, HEAD_DIM, rows), lambda j, info, slot: (j, 0, 0)),
    ]
    out_shape = jax.ShapeDtypeStruct(queries.shape, queries.dtype)
    out_spec = pl.BlockSpec((span_len, heads * HEAD_DIM), lambda j, info, slot: (j, 0))
    state = None
    base = 0
    for index, piece in enumerate(pieces):
        first = index == 0
        last = index == len(pieces) - 1
        share = piece.shape[0] / n_spans
        kernel = functools.partial(
            attend_kernel, heads=heads, span_len=span_len, scale=HEAD_DIM ** (-0.5),
            base=base, first=first, last=last,
        )
        cost = pl.CostEstimate(
            flops=int(4 * rows * span_len * HEAD_DIM * blocks_est * share),
            transcendentals=int(rows * span_len * blocks_est * share),
            bytes_accessed=2 * queries.size * 2 + piece.size * 2 + 16 * n_local * HEAD_DIM * rows,
        )
        in_specs = [
            pl.BlockSpec((None, HEAD_DIM, rows), lambda j, info, slot: (j, 0, 0)),
            pl.BlockSpec(piece.shape, lambda j, info, slot: (0, 0, 0)),
            pl.BlockSpec((None, 1, span_len), lambda j, info, slot: (j, 0, 0)),
        ]
        operands = [info, where_held, q_t, piece, doc_rows]
        if not first:
            in_specs = in_specs + state_specs
            operands = operands + list(state)
        if last:
            out_shapes, out_specs = out_shape, out_spec
        else:
            out_shapes, out_specs = state_shapes, state_specs
        grid_spec = pltpu.PrefetchScalarGridSpec(
            num_scalar_prefetch=2,
            grid=(n_local,),
            in_specs=in_specs,
            out_specs=out_specs,
            scratch_shapes=[
                pltpu.VMEM((1, rows), jnp.float32),
                pltpu.VMEM((1, rows), jnp.float32),
                pltpu.VMEM((HEAD_DIM, rows), jnp.float32),
            ],
        )
        result = pl.pallas_call(
            kernel,
            grid_spec=grid_spec,
            out_shape=out_shapes,
            compiler_params=pltpu.CompilerParams(dimension_semantics=("arbitrary",)),
            cost_estimate=cost,
        )(*operands)
        base += piece.shape[0]
        if last:
            return result
        state = result


def solution(mesh):
    in_specs = (P("ctx", "head"), P(("ctx", "head"), None), P(("ctx", "head"), None), P(), P("ctx"))
    out_specs = P("ctx", "head")
    return jax.shard_map(
        on_device, mesh=mesh, in_specs=in_specs, out_specs=out_specs, check_vma=False
    )
```

```python
import functools

import jax
import jax.numpy as jnp
from jax import lax
from jax.experimental import pallas as pl
from jax.experimental.pallas import tpu as pltpu
from jax.sharding import PartitionSpec as P


HEAD_DIM = 128


NEG = -1e30

ORDER_CORE0 = (4, 3, 2, 0)
ORDER_CORE1 = (0, 2, 4, 3)
CORE_BIT = 1


def doubling_gather(block, flat_index, n_dev):
    core = (flat_index >> CORE_BIT) & 1
    held = block
    pieces = []
    for step in range(len(ORDER_CORE0)):
        pairs = []
        for k in range(n_dev):
            bit = ORDER_CORE0[step] if ((k >> CORE_BIT) & 1) == 0 else ORDER_CORE1[step]
            pairs.append((k, k ^ (1 << bit)))
        other = lax.ppermute(held, ("ctx", "head"), pairs)
        if step == len(ORDER_CORE0) - 1:
            pieces.append(held)
            pieces.append(other)
        held = jnp.concatenate([held, other], axis=0)
    other = lax.ppermute(held, ("ctx", "head"), [(k, k ^ (1 << CORE_BIT)) for k in range(n_dev)])
    pieces.append(other)

    def source_mask(order, j):
        mask = 0
        for t, bit in enumerate(order):
            mask = mask | (((j >> t) & 1) << bit)
        return mask

    half = 1 << len(ORDER_CORE0)
    j = jnp.arange(2 * half, dtype=jnp.int32)
    jl = j % half
    own_order_mask = jnp.where(core == 0, source_mask(ORDER_CORE0, jl), source_mask(ORDER_CORE1, jl))
    partner_order_mask = jnp.where(
        core == 0, source_mask(ORDER_CORE1, jl), source_mask(ORDER_CORE0, jl)
    )
    partner = flat_index ^ (1 << CORE_BIT)
    source = jnp.where(j < half, flat_index ^ own_order_mask, partner ^ partner_order_mask)
    return pieces, source


def attend_kernel(info_ref, slot_ref, qt_ref, kv_ref, doc_ref, *rest,
                  heads, span_len, scale, base, first, last):
    rest = list(rest)
    if not first:
        im_ref, il_ref, iacc_ref = rest[:3]
        rest = rest[3:]
    if last:
        o_ref = rest[0]
        rest = rest[1:]
    else:
        om_ref, ol_ref, oacc_ref = rest[:3]
        rest = rest[3:]
    m_ref, l_ref, acc_ref = rest
    j = pl.program_id(0)
    own = info_ref[0, j]
    low = info_ref[1, j]
    full_low = jnp.minimum(info_ref[2, j], own)
    count = kv_ref.shape[0]
    rows = heads * span_len

    if first:
        m_ref[...] = jnp.full(m_ref.shape, NEG, jnp.float32)
        l_ref[...] = jnp.zeros(l_ref.shape, jnp.float32)
        acc_ref[...] = jnp.zeros(acc_ref.shape, jnp.float32)
    else:
        m_ref[...] = im_ref[...]
        l_ref[...] = il_ref[...]
        acc_ref[...] = iacc_ref[...]

    doc_row = doc_ref[...]
    doc = jnp.concatenate([doc_row] * heads, axis=1)
    cols = lax.broadcasted_iota(jnp.int32, (1, rows), 1)
    qpos = own * span_len + lax.rem(cols, span_len)

    def block(p, masked):
        b = slot_ref[p] - base

        @pl.when((b >= 0) & (b < count))
        def _():
            kv = kv_ref[b]
            keys = kv[:, :HEAD_DIM]
            vals_t = kv[:, HEAD_DIM:]
            scores = jnp.dot(keys, qt_ref[...], preferred_element_type=jnp.float32)
            if masked:
                kpos = p * span_len + lax.broadcasted_iota(jnp.int32, (span_len, 1), 0)
                visible = (kpos >= doc) & (kpos <= qpos)
                scores = jnp.where(visible, scores, NEG)
            old_max = m_ref[...]
            new_max = jnp.maximum(old_max, jnp.max(scores, axis=0, keepdims=True))
            rescale = jnp.exp((old_max - new_max) * scale)
            weights = jnp.exp((scores - new_max) * scale)
            if masked:
                weights = jnp.where(visible, weights, 0.0)
            sums = jnp.sum(weights, axis=0, keepdims=True)
            mixed = jnp.dot(vals_t, weights.astype(jnp.bfloat16), preferred_element_type=jnp.float32)
            l_ref[...] = rescale * l_ref[...] + sums
            acc_ref[...] = rescale * acc_ref[...] + mixed
            m_ref[...] = new_max

    block(own, True)

    def masked_step(p, carry):
        block(p, True)
        return carry

    def full_step(p, carry):
        block(p, False)
        return carry

    lax.fori_loop(low, full_low, masked_step, 0)
    lax.fori_loop(jnp.maximum(full_low, low), own, full_step, 0)

    if last:
        out_t = acc_ref[...] / l_ref[...]
        for h in range(heads):
            o_ref[:, h * HEAD_DIM:(h + 1) * HEAD_DIM] = out_t[
                :, h * span_len:(h + 1) * span_len
            ].T.astype(o_ref.dtype)
    else:
        om_ref[...] = m_ref[...]
        ol_ref[...] = l_ref[...]
        oacc_ref[...] = acc_ref[...]


def span_blocks(keys, vals, span_len):
    n = keys.shape[0] // span_len
    vals_t = jnp.swapaxes(vals.reshape(n, span_len, HEAD_DIM), 1, 2)
    return jnp.concatenate([keys.reshape(n, span_len, HEAD_DIM), vals_t], axis=2)


def attend_all(queries, key_rows, value_rows, span_order, doc_start):
    tok_rows = queries.shape[0]
    heads = queries.shape[1] // HEAD_DIM
    kv_count = key_rows.shape[1] // HEAD_DIM
    n_ctx = lax.axis_size("ctx")
    n_head = lax.axis_size("head")
    n_dev = n_ctx * n_head
    ctx_index = lax.axis_index("ctx")
    n_spans = span_order.shape[0]
    length = key_rows.shape[0] * n_dev
    span_len = length // n_spans
    n_local = tok_rows // span_len
    group_index = lax.axis_index("head") * kv_count // n_head
    slot_ids = jnp.arange(n_spans, dtype=jnp.int32)

    if kv_count == 1 and n_dev == 32 and key_rows.shape[0] == span_len:
        flat_index = ctx_index * n_head + lax.axis_index("head")
        local = span_blocks(key_rows, value_rows, span_len)
        pieces, source = doubling_gather(local, flat_index, n_dev)
    else:
        both = jnp.concatenate([key_rows, value_rows], axis=1)
        block_rows = lax.all_gather(both, "head", axis=0, tiled=True)
        own_keys = lax.dynamic_slice_in_dim(block_rows, group_index * HEAD_DIM, HEAD_DIM, 1)
        own_vals = lax.dynamic_slice_in_dim(
            block_rows, (kv_count + group_index) * HEAD_DIM, HEAD_DIM, 1
        )
        local = span_blocks(own_keys, own_vals, span_len)
        whole = lax.all_gather(local, "ctx", axis=0, tiled=True)
        pieces = [whole]
        source = slot_ids

    inverse = jnp.sum(
        jnp.where(span_order[None, :] == slot_ids[:, None], slot_ids[None, :], 0), axis=1
    ).astype(jnp.int32)
    where_held = jnp.sum(
        jnp.where(inverse[:, None] == source[None, :], slot_ids[None, :], 0), axis=1
    ).astype(jnp.int32)

    local_slots = ctx_index * n_local + jnp.arange(n_local, dtype=jnp.int32)
    own_span = jnp.sum(
        jnp.where(local_slots[:, None] == slot_ids[None, :], span_order[None, :], 0), axis=1
    ).astype(jnp.int32)
    doc_spans = doc_start.reshape(n_local, span_len)
    low = jnp.min(doc_spans, axis=1) // span_len
    full_low = (jnp.max(doc_spans, axis=1) + span_len - 1) // span_len
    info = jnp.stack([own_span, low, full_low]).astype(jnp.int32)

    rows = heads * span_len
    doc_rows = doc_start.reshape(n_local, 1, span_len)
    q_t = jnp.transpose(
        queries.reshape(n_local, span_len, heads, HEAD_DIM), (0, 3, 2, 1)
    ).reshape(n_local, HEAD_DIM, rows)

    blocks_est = n_local * (n_spans // 2 + 1)
    state_shapes = [
        jax.ShapeDtypeStruct((n_local, 1, rows), jnp.float32),
        jax.ShapeDtypeStruct((n_local, 1, rows), jnp.float32),
        jax.ShapeDtypeStruct((n_local, HEAD_DIM, rows), jnp.float32),
    ]
    state_specs = [
        pl.BlockSpec((None, 1, rows), lambda j, info, slot: (j, 0, 0)),
        pl.BlockSpec((None, 1, rows), lambda j, info, slot: (j, 0, 0)),
        pl.BlockSpec((None, HEAD_DIM, rows), lambda j, info, slot: (j, 0, 0)),
    ]
    out_shape = jax.ShapeDtypeStruct(queries.shape, queries.dtype)
    out_spec = pl.BlockSpec((span_len, heads * HEAD_DIM), lambda j, info, slot: (j, 0))
    state = None
    base = 0
    for index, piece in enumerate(pieces):
        first = index == 0
        last = index == len(pieces) - 1
        share = piece.shape[0] / n_spans
        kernel = functools.partial(
            attend_kernel, heads=heads, span_len=span_len, scale=HEAD_DIM ** (-0.5),
            base=base, first=first, last=last,
        )
        cost = pl.CostEstimate(
            flops=int(4 * rows * span_len * HEAD_DIM * blocks_est * share),
            transcendentals=int(rows * span_len * blocks_est * share),
            bytes_accessed=2 * queries.size * 2 + piece.size * 2 + 16 * n_local * HEAD_DIM * rows,
        )
        in_specs = [
            pl.BlockSpec((None, HEAD_DIM, rows), lambda j, info, slot: (j, 0, 0)),
            pl.BlockSpec(piece.shape, lambda j, info, slot: (0, 0, 0)),
            pl.BlockSpec((None, 1, span_len), lambda j, info, slot: (j, 0, 0)),
        ]
        operands = [info, where_held, q_t, piece, doc_rows]
        if not first:
            in_specs = in_specs + state_specs
            operands = operands + list(state)
        if last:
            out_shapes, out_specs = out_shape, out_spec
        else:
            out_shapes, out_specs = state_shapes, state_specs
        grid_spec = pltpu.PrefetchScalarGridSpec(
            num_scalar_prefetch=2,
            grid=(n_local,),
            in_specs=in_specs,
            out_specs=out_specs,
            scratch_shapes=[
                pltpu.VMEM((1, rows), jnp.float32),
                pltpu.VMEM((1, rows), jnp.float32),
                pltpu.VMEM((HEAD_DIM, rows), jnp.float32),
            ],
        )
        result = pl.pallas_call(
            kernel,
            grid_spec=grid_spec,
            out_shape=out_shapes,
            compiler_params=pltpu.CompilerParams(dimension_semantics=("arbitrary",)),
            cost_estimate=cost,
        )(*operands)
        base += piece.shape[0]
        if last:
            return result
        state = result


def solution(mesh):
    in_specs = (P("ctx", "head"), P(("ctx", "head"), None), P(("ctx", "head"), None), P(), P("ctx"))
    out_specs = P("ctx", "head")
    return jax.shard_map(
        attend_all, mesh=mesh, in_specs=in_specs, out_specs=out_specs, check_vma=False
    )
```

```python
import functools

import jax
import jax.numpy as jnp
from jax import lax
from jax.experimental import pallas as pl
from jax.experimental.pallas import tpu as pltpu
from jax.sharding import PartitionSpec as P


HEAD_DIM = 128


NEG = -1e30

ORDER_CORE0 = (4, 3, 2, 0)
ORDER_CORE1 = (0, 2, 4, 3)
CORE_BIT = 1


def doubling_gather(block, flat_index, n_dev):
    core = (flat_index >> CORE_BIT) & 1
    held = block
    pieces = []
    for step in range(len(ORDER_CORE0)):
        pairs = []
        for k in range(n_dev):
            bit = ORDER_CORE0[step] if ((k >> CORE_BIT) & 1) == 0 else ORDER_CORE1[step]
            pairs.append((k, k ^ (1 << bit)))
        other = lax.ppermute(held, ("ctx", "head"), pairs)
        if step == len(ORDER_CORE0) - 1:
            pieces.append(held)
            pieces.append(other)
        held = jnp.concatenate([held, other], axis=0)
    other = lax.ppermute(held, ("ctx", "head"), [(k, k ^ (1 << CORE_BIT)) for k in range(n_dev)])
    pieces.append(other)

    def source_mask(order, j):
        mask = 0
        for t, bit in enumerate(order):
            mask = mask | (((j >> t) & 1) << bit)
        return mask

    half = 1 << len(ORDER_CORE0)
    j = jnp.arange(2 * half, dtype=jnp.int32)
    jl = j % half
    own_order_mask = jnp.where(core == 0, source_mask(ORDER_CORE0, jl), source_mask(ORDER_CORE1, jl))
    partner_order_mask = jnp.where(
        core == 0, source_mask(ORDER_CORE1, jl), source_mask(ORDER_CORE0, jl)
    )
    partner = flat_index ^ (1 << CORE_BIT)
    source = jnp.where(j < half, flat_index ^ own_order_mask, partner ^ partner_order_mask)
    return pieces, source


def attend_kernel(info_ref, slot_ref, qt_ref, kv_ref, doc_ref, *rest,
                  heads, span_len, scale, base, first, last, n_local):
    rest = list(rest)
    if not first:
        im_all, il_all, iacc_all = rest[:3]
        rest = rest[3:]
    m_all, l_all, acc_all = rest[:3]
    o_ref = rest[3] if last else None
    count = kv_ref.shape[0]
    rows = heads * span_len
    cols = lax.broadcasted_iota(jnp.int32, (1, rows), 1)

    for j in range(n_local):
        own = info_ref[0, j]
        low = info_ref[1, j]
        full_low = jnp.minimum(info_ref[2, j], own)
        m_ref = m_all.at[j]
        l_ref = l_all.at[j]
        acc_ref = acc_all.at[j]
        qt_ref_j = qt_ref.at[j]

        if first:
            m_ref[...] = jnp.full(m_ref.shape, NEG, jnp.float32)
            l_ref[...] = jnp.zeros(l_ref.shape, jnp.float32)
            acc_ref[...] = jnp.zeros(acc_ref.shape, jnp.float32)
        else:
            m_ref[...] = im_all[j]
            l_ref[...] = il_all[j]
            acc_ref[...] = iacc_all[j]

        doc = jnp.concatenate([doc_ref[j]] * heads, axis=1)
        qpos = own * span_len + lax.rem(cols, span_len)

        def block(p, masked, m_ref=m_ref, l_ref=l_ref, acc_ref=acc_ref, qt_ref_j=qt_ref_j,
                  doc=doc, qpos=qpos):
            b = slot_ref[p] - base

            @pl.when((b >= 0) & (b < count))
            def _():
                kv = kv_ref[b]
                keys = kv[:, :HEAD_DIM]
                vals_t = kv[:, HEAD_DIM:]
                scores = jnp.dot(keys, qt_ref_j[...], preferred_element_type=jnp.float32)
                if masked:
                    kpos = p * span_len + lax.broadcasted_iota(jnp.int32, (span_len, 1), 0)
                    visible = (kpos >= doc) & (kpos <= qpos)
                    scores = jnp.where(visible, scores, NEG)
                old_max = m_ref[...]
                new_max = jnp.maximum(old_max, jnp.max(scores, axis=0, keepdims=True))
                rescale = jnp.exp((old_max - new_max) * scale)
                weights = jnp.exp((scores - new_max) * scale)
                if masked:
                    weights = jnp.where(visible, weights, 0.0)
                sums = jnp.sum(weights, axis=0, keepdims=True)
                mixed = jnp.dot(vals_t, weights.astype(jnp.bfloat16), preferred_element_type=jnp.float32)
                l_ref[...] = rescale * l_ref[...] + sums
                acc_ref[...] = rescale * acc_ref[...] + mixed
                m_ref[...] = new_max

        block(own, True)

        def masked_step(p, carry, block=block):
            block(p, True)
            return carry

        def full_step(p, carry, block=block):
            block(p, False)
            return carry

        lax.fori_loop(low, full_low, masked_step, 0)
        lax.fori_loop(jnp.maximum(full_low, low), own, full_step, 0)

        if last:
            out_t = acc_ref[...] / l_ref[...]
            for h in range(heads):
                o_ref[j * span_len:(j + 1) * span_len, h * HEAD_DIM:(h + 1) * HEAD_DIM] = out_t[
                    :, h * span_len:(h + 1) * span_len
                ].T.astype(o_ref.dtype)


def span_blocks(keys, vals, span_len):
    n = keys.shape[0] // span_len
    vals_t = jnp.swapaxes(vals.reshape(n, span_len, HEAD_DIM), 1, 2)
    return jnp.concatenate([keys.reshape(n, span_len, HEAD_DIM), vals_t], axis=2)


def attend_all(queries, key_rows, value_rows, span_order, doc_start):
    tok_rows = queries.shape[0]
    heads = queries.shape[1] // HEAD_DIM
    kv_count = key_rows.shape[1] // HEAD_DIM
    n_ctx = lax.axis_size("ctx")
    n_head = lax.axis_size("head")
    n_dev = n_ctx * n_head
    ctx_index = lax.axis_index("ctx")
    n_spans = span_order.shape[0]
    length = key_rows.shape[0] * n_dev
    span_len = length // n_spans
    n_local = tok_rows // span_len
    group_index = lax.axis_index("head") * kv_count // n_head
    slot_ids = jnp.arange(n_spans, dtype=jnp.int32)

    if kv_count == 1 and n_dev == 32 and key_rows.shape[0] == span_len:
        flat_index = ctx_index * n_head + lax.axis_index("head")
        local = span_blocks(key_rows, value_rows, span_len)
        pieces, source = doubling_gather(local, flat_index, n_dev)
    else:
        both = jnp.concatenate([key_rows, value_rows], axis=1)
        block_rows = lax.all_gather(both, "head", axis=0, tiled=True)
        own_keys = lax.dynamic_slice_in_dim(block_rows, group_index * HEAD_DIM, HEAD_DIM, 1)
        own_vals = lax.dynamic_slice_in_dim(
            block_rows, (kv_count + group_index) * HEAD_DIM, HEAD_DIM, 1
        )
        local = span_blocks(own_keys, own_vals, span_len)
        whole = lax.all_gather(local, "ctx", axis=0, tiled=True)
        pieces = [whole]
        source = slot_ids

    inverse = jnp.sum(
        jnp.where(span_order[None, :] == slot_ids[:, None], slot_ids[None, :], 0), axis=1
    ).astype(jnp.int32)
    where_held = jnp.sum(
        jnp.where(inverse[:, None] == source[None, :], slot_ids[None, :], 0), axis=1
    ).astype(jnp.int32)

    local_slots = ctx_index * n_local + jnp.arange(n_local, dtype=jnp.int32)
    own_span = jnp.sum(
        jnp.where(local_slots[:, None] == slot_ids[None, :], span_order[None, :], 0), axis=1
    ).astype(jnp.int32)
    doc_spans = doc_start.reshape(n_local, span_len)
    low = jnp.min(doc_spans, axis=1) // span_len
    full_low = (jnp.max(doc_spans, axis=1) + span_len - 1) // span_len
    info = jnp.stack([own_span, low, full_low]).astype(jnp.int32)

    rows = heads * span_len
    doc_rows = doc_start.reshape(n_local, 1, span_len)
    q_t = jnp.transpose(
        queries.reshape(n_local, span_len, heads, HEAD_DIM), (0, 3, 2, 1)
    ).reshape(n_local, HEAD_DIM, rows)

    blocks_est = n_local * (n_spans // 2 + 1)
    state_shapes = [
        jax.ShapeDtypeStruct((n_local, 1, rows), jnp.float32),
        jax.ShapeDtypeStruct((n_local, 1, rows), jnp.float32),
        jax.ShapeDtypeStruct((n_local, HEAD_DIM, rows), jnp.float32),
    ]
    out_shape = jax.ShapeDtypeStruct(queries.shape, queries.dtype)
    vmem = pl.BlockSpec(memory_space=pltpu.VMEM)
    smem = pl.BlockSpec(memory_space=pltpu.SMEM)
    state = None
    base = 0
    for index, piece in enumerate(pieces):
        first = index == 0
        last = index == len(pieces) - 1
        share = piece.shape[0] / n_spans
        kernel = functools.partial(
            attend_kernel, heads=heads, span_len=span_len, scale=HEAD_DIM ** (-0.5),
            base=base, first=first, last=last, n_local=n_local,
        )
        cost = pl.CostEstimate(
            flops=int(4 * rows * span_len * HEAD_DIM * blocks_est * share),
            transcendentals=int(rows * span_len * blocks_est * share),
            bytes_accessed=2 * queries.size * 2 + piece.size * 2,
        )
        operands = [info, where_held, q_t, piece, doc_rows]
        in_specs = [smem, smem, vmem, vmem, vmem]
        if not first:
            operands = operands + list(state)
            in_specs = in_specs + [vmem] * 3
        out_shapes = list(state_shapes) + ([out_shape] if last else [])
        result = pl.pallas_call(
            kernel,
            in_specs=in_specs,
            out_specs=[vmem] * len(out_shapes),
            out_shape=out_shapes,
            cost_estimate=cost,
        )(*operands)
        base += piece.shape[0]
        if last:
            return result[3]
        state = result[:3]


def solution(mesh):
    in_specs = (P("ctx", "head"), P(("ctx", "head"), None), P(("ctx", "head"), None), P(), P("ctx"))
    out_specs = P("ctx", "head")
    return jax.shard_map(
        attend_all, mesh=mesh, in_specs=in_specs, out_specs=out_specs, check_vma=False
    )
```

```python
import functools

import jax
import jax.numpy as jnp
from jax import lax
from jax.experimental import pallas as pl
from jax.experimental.pallas import tpu as pltpu
from jax.sharding import PartitionSpec as P


HEAD_DIM = 128


NEG = -1e30
LOG2_E = 1.4426950408889634

ORDER_CORE0 = (4, 3, 2, 0)
ORDER_CORE1 = (0, 2, 4, 3)
CORE_BIT = 1


def doubling_gather(block, flat_index, n_dev):
    core = (flat_index >> CORE_BIT) & 1
    held = block
    pieces = []
    for step in range(len(ORDER_CORE0)):
        pairs = []
        for k in range(n_dev):
            bit = ORDER_CORE0[step] if ((k >> CORE_BIT) & 1) == 0 else ORDER_CORE1[step]
            pairs.append((k, k ^ (1 << bit)))
        other = lax.ppermute(held, ("ctx", "head"), pairs)
        if step == len(ORDER_CORE0) - 1:
            pieces.append(held)
            pieces.append(other)
        held = jnp.concatenate([held, other], axis=0)
    other = lax.ppermute(held, ("ctx", "head"), [(k, k ^ (1 << CORE_BIT)) for k in range(n_dev)])
    pieces.append(other)

    def source_mask(order, j):
        mask = 0
        for t, bit in enumerate(order):
            mask = mask | (((j >> t) & 1) << bit)
        return mask

    half = 1 << len(ORDER_CORE0)
    j = jnp.arange(2 * half, dtype=jnp.int32)
    jl = j % half
    own_order_mask = jnp.where(core == 0, source_mask(ORDER_CORE0, jl), source_mask(ORDER_CORE1, jl))
    partner_order_mask = jnp.where(
        core == 0, source_mask(ORDER_CORE1, jl), source_mask(ORDER_CORE0, jl)
    )
    partner = flat_index ^ (1 << CORE_BIT)
    source = jnp.where(j < half, flat_index ^ own_order_mask, partner ^ partner_order_mask)
    return pieces, source


def attend_kernel(info_ref, slot_ref, qt_ref, kv_ref, doc_ref, *rest,
                  heads, span_len, scale, base, first, last, n_local):
    rest = list(rest)
    if not first:
        im_all, il_all, iacc_all = rest[:3]
        rest = rest[3:]
    m_all, l_all, acc_all = rest[:3]
    o_ref = rest[3] if last else None
    count = kv_ref.shape[0]
    rows = heads * span_len
    cols = lax.broadcasted_iota(jnp.int32, (1, rows), 1)

    for j in range(n_local):
        own = info_ref[0, j]
        low = info_ref[1, j]
        full_low = jnp.minimum(info_ref[2, j], own)
        m_ref = m_all.at[j]
        l_ref = l_all.at[j]
        acc_ref = acc_all.at[j]
        qt_ref_j = qt_ref.at[j]

        if first:
            m_ref[...] = jnp.full(m_ref.shape, NEG, jnp.float32)
            l_ref[...] = jnp.zeros(l_ref.shape, jnp.float32)
            acc_ref[...] = jnp.zeros(acc_ref.shape, jnp.float32)
        else:
            m_ref[...] = im_all[j]
            l_ref[...] = il_all[j]
            acc_ref[...] = iacc_all[j]

        doc = jnp.concatenate([doc_ref[j]] * heads, axis=1)
        qpos = own * span_len + lax.rem(cols, span_len)

        def block(p, masked, m_ref=m_ref, l_ref=l_ref, acc_ref=acc_ref, qt_ref_j=qt_ref_j,
                  doc=doc, qpos=qpos):
            b = slot_ref[p] - base

            @pl.when((b >= 0) & (b < count))
            def _():
                kv = kv_ref[b]
                keys = kv[:, :HEAD_DIM]
                vals_t = kv[:, HEAD_DIM:]
                scores = jnp.dot(keys, qt_ref_j[...], preferred_element_type=jnp.float32)
                if masked:
                    kpos = p * span_len + lax.broadcasted_iota(jnp.int32, (span_len, 1), 0)
                    visible = (kpos >= doc) & (kpos <= qpos)
                    scores = jnp.where(visible, scores, NEG)
                old_max = m_ref[...]
                new_max = jnp.maximum(old_max, jnp.max(scores, axis=0, keepdims=True))
                rescale = jnp.exp2((old_max - new_max) * scale)
                weights = jnp.exp2((scores - new_max) * scale)
                if masked:
                    weights = jnp.where(visible, weights, 0.0)
                sums = jnp.sum(weights, axis=0, keepdims=True)
                mixed = jnp.dot(vals_t, weights.astype(jnp.bfloat16), preferred_element_type=jnp.float32)
                l_ref[...] = rescale * l_ref[...] + sums
                acc_ref[...] = rescale * acc_ref[...] + mixed
                m_ref[...] = new_max

        block(own, True)

        def masked_step(p, carry, block=block):
            block(p, True)
            return carry

        def full_step(p, carry, block=block):
            block(p, False)
            return carry

        lax.fori_loop(low, full_low, masked_step, 0)
        lax.fori_loop(jnp.maximum(full_low, low), own, full_step, 0)

        if last:
            out_t = acc_ref[...] / l_ref[...]
            for h in range(heads):
                o_ref[j * span_len:(j + 1) * span_len, h * HEAD_DIM:(h + 1) * HEAD_DIM] = out_t[
                    :, h * span_len:(h + 1) * span_len
                ].T.astype(o_ref.dtype)


def span_blocks(keys, vals, span_len):
    n = keys.shape[0] // span_len
    vals_t = jnp.swapaxes(vals.reshape(n, span_len, HEAD_DIM), 1, 2)
    return jnp.concatenate([keys.reshape(n, span_len, HEAD_DIM), vals_t], axis=2)


def attend_all(queries, key_rows, value_rows, span_order, doc_start):
    tok_rows = queries.shape[0]
    heads = queries.shape[1] // HEAD_DIM
    kv_count = key_rows.shape[1] // HEAD_DIM
    n_ctx = lax.axis_size("ctx")
    n_head = lax.axis_size("head")
    n_dev = n_ctx * n_head
    ctx_index = lax.axis_index("ctx")
    n_spans = span_order.shape[0]
    length = key_rows.shape[0] * n_dev
    span_len = length // n_spans
    n_local = tok_rows // span_len
    group_index = lax.axis_index("head") * kv_count // n_head
    slot_ids = jnp.arange(n_spans, dtype=jnp.int32)

    if kv_count == 1 and n_dev == 32 and key_rows.shape[0] == span_len:
        flat_index = ctx_index * n_head + lax.axis_index("head")
        local = span_blocks(key_rows, value_rows, span_len)
        pieces, source = doubling_gather(local, flat_index, n_dev)
    else:
        both = jnp.concatenate([key_rows, value_rows], axis=1)
        block_rows = lax.all_gather(both, "head", axis=0, tiled=True)
        own_keys = lax.dynamic_slice_in_dim(block_rows, group_index * HEAD_DIM, HEAD_DIM, 1)
        own_vals = lax.dynamic_slice_in_dim(
            block_rows, (kv_count + group_index) * HEAD_DIM, HEAD_DIM, 1
        )
        local = span_blocks(own_keys, own_vals, span_len)
        whole = lax.all_gather(local, "ctx", axis=0, tiled=True)
        pieces = [whole]
        source = slot_ids

    inverse = jnp.sum(
        jnp.where(span_order[None, :] == slot_ids[:, None], slot_ids[None, :], 0), axis=1
    ).astype(jnp.int32)
    where_held = jnp.sum(
        jnp.where(inverse[:, None] == source[None, :], slot_ids[None, :], 0), axis=1
    ).astype(jnp.int32)

    local_slots = ctx_index * n_local + jnp.arange(n_local, dtype=jnp.int32)
    own_span = jnp.sum(
        jnp.where(local_slots[:, None] == slot_ids[None, :], span_order[None, :], 0), axis=1
    ).astype(jnp.int32)
    doc_spans = doc_start.reshape(n_local, span_len)
    low = jnp.min(doc_spans, axis=1) // span_len
    full_low = (jnp.max(doc_spans, axis=1) + span_len - 1) // span_len
    info = jnp.stack([own_span, low, full_low]).astype(jnp.int32)

    rows = heads * span_len
    doc_rows = doc_start.reshape(n_local, 1, span_len)
    q_t = jnp.transpose(
        queries.reshape(n_local, span_len, heads, HEAD_DIM), (0, 3, 2, 1)
    ).reshape(n_local, HEAD_DIM, rows)

    blocks_est = n_local * (n_spans // 2 + 1)
    state_shapes = [
        jax.ShapeDtypeStruct((n_local, 1, rows), jnp.float32),
        jax.ShapeDtypeStruct((n_local, 1, rows), jnp.float32),
        jax.ShapeDtypeStruct((n_local, HEAD_DIM, rows), jnp.float32),
    ]
    out_shape = jax.ShapeDtypeStruct(queries.shape, queries.dtype)
    vmem = pl.BlockSpec(memory_space=pltpu.VMEM)
    smem = pl.BlockSpec(memory_space=pltpu.SMEM)
    state = None
    base = 0
    for index, piece in enumerate(pieces):
        first = index == 0
        last = index == len(pieces) - 1
        share = piece.shape[0] / n_spans
        kernel = functools.partial(
            attend_kernel, heads=heads, span_len=span_len, scale=HEAD_DIM ** (-0.5) * LOG2_E,
            base=base, first=first, last=last, n_local=n_local,
        )
        cost = pl.CostEstimate(
            flops=int(4 * rows * span_len * HEAD_DIM * blocks_est * share),
            transcendentals=int(rows * span_len * blocks_est * share),
            bytes_accessed=2 * queries.size * 2 + piece.size * 2,
        )
        operands = [info, where_held, q_t, piece, doc_rows]
        in_specs = [smem, smem, vmem, vmem, vmem]
        if not first:
            operands = operands + list(state)
            in_specs = in_specs + [vmem] * 3
        out_shapes = list(state_shapes) + ([out_shape] if last else [])
        result = pl.pallas_call(
            kernel,
            in_specs=in_specs,
            out_specs=[vmem] * len(out_shapes),
            out_shape=out_shapes,
            cost_estimate=cost,
        )(*operands)
        base += piece.shape[0]
        if last:
            return result[3]
        state = result[:3]


def solution(mesh):
    in_specs = (P("ctx", "head"), P(("ctx", "head"), None), P(("ctx", "head"), None), P(), P("ctx"))
    out_specs = P("ctx", "head")
    return jax.shard_map(
        attend_all, mesh=mesh, in_specs=in_specs, out_specs=out_specs, check_vma=False
    )
```

```python
import functools

import jax
import jax.numpy as jnp
from jax import lax
from jax.experimental import pallas as pl
from jax.experimental.pallas import tpu as pltpu
from jax.sharding import PartitionSpec as P


HEAD_DIM = 128


NEG = -1e30
LOG2_E = 1.4426950408889634

ORDER_CORE0 = (4, 3, 2, 0)
ORDER_CORE1 = (0, 2, 4, 3)
CORE_BIT = 1


def doubling_gather(block, flat_index, n_dev):
    core = (flat_index >> CORE_BIT) & 1
    held = block
    pieces = []
    for step in range(len(ORDER_CORE0)):
        pairs = []
        for k in range(n_dev):
            bit = ORDER_CORE0[step] if ((k >> CORE_BIT) & 1) == 0 else ORDER_CORE1[step]
            pairs.append((k, k ^ (1 << bit)))
        other = lax.ppermute(held, ("ctx", "head"), pairs)
        if step == len(ORDER_CORE0) - 1:
            pieces.append(held)
            pieces.append(other)
            held = (held, other)
        else:
            held = jnp.concatenate([held, other], axis=0)
    other = lax.ppermute(held, ("ctx", "head"), [(k, k ^ (1 << CORE_BIT)) for k in range(n_dev)])
    pieces.append(tuple(other))

    def source_mask(order, j):
        mask = 0
        for t, bit in enumerate(order):
            mask = mask | (((j >> t) & 1) << bit)
        return mask

    half = 1 << len(ORDER_CORE0)
    j = jnp.arange(2 * half, dtype=jnp.int32)
    jl = j % half
    own_order_mask = jnp.where(core == 0, source_mask(ORDER_CORE0, jl), source_mask(ORDER_CORE1, jl))
    partner_order_mask = jnp.where(
        core == 0, source_mask(ORDER_CORE1, jl), source_mask(ORDER_CORE0, jl)
    )
    partner = flat_index ^ (1 << CORE_BIT)
    source = jnp.where(j < half, flat_index ^ own_order_mask, partner ^ partner_order_mask)
    return pieces, source


def attend_kernel(info_ref, slot_ref, qt_ref, *rest,
                  heads, span_len, scale, base, first, last, n_local, n_kv):
    rest = list(rest)
    kv_refs = rest[:n_kv]
    doc_ref = rest[n_kv]
    rest = rest[n_kv + 1:]
    if not first:
        im_all, il_all, iacc_all = rest[:3]
        rest = rest[3:]
    m_all, l_all, acc_all = rest[:3]
    o_ref = rest[3] if last else None
    count = sum(r.shape[0] for r in kv_refs)

    def load_kv(b):
        kv = kv_refs[0][jnp.minimum(b, kv_refs[0].shape[0] - 1)]
        offset = kv_refs[0].shape[0]
        for r in kv_refs[1:]:
            here = r[jnp.clip(b - offset, 0, r.shape[0] - 1)]
            kv = jnp.where(b >= offset, here, kv)
            offset += r.shape[0]
        return kv

    rows = heads * span_len
    cols = lax.broadcasted_iota(jnp.int32, (1, rows), 1)

    for j in range(n_local):
        own = info_ref[0, j]
        low = info_ref[1, j]
        full_low = jnp.minimum(info_ref[2, j], own)
        m_ref = m_all.at[j]
        l_ref = l_all.at[j]
        acc_ref = acc_all.at[j]
        qt_ref_j = qt_ref.at[j]

        if first:
            m_ref[...] = jnp.full(m_ref.shape, NEG, jnp.float32)
            l_ref[...] = jnp.zeros(l_ref.shape, jnp.float32)
            acc_ref[...] = jnp.zeros(acc_ref.shape, jnp.float32)
        else:
            m_ref[...] = im_all[j]
            l_ref[...] = il_all[j]
            acc_ref[...] = iacc_all[j]

        doc = jnp.concatenate([doc_ref[j]] * heads, axis=1)
        qpos = own * span_len + lax.rem(cols, span_len)

        def block(p, masked, m_ref=m_ref, l_ref=l_ref, acc_ref=acc_ref, qt_ref_j=qt_ref_j,
                  doc=doc, qpos=qpos):
            b = slot_ref[p] - base

            @pl.when((b >= 0) & (b < count))
            def _():
                kv = load_kv(b)
                keys = kv[:, :HEAD_DIM]
                vals_t = kv[:, HEAD_DIM:]
                scores = jnp.dot(keys, qt_ref_j[...], preferred_element_type=jnp.float32)
                if masked:
                    kpos = p * span_len + lax.broadcasted_iota(jnp.int32, (span_len, 1), 0)
                    visible = (kpos >= doc) & (kpos <= qpos)
                    scores = jnp.where(visible, scores, NEG)
                old_max = m_ref[...]
                new_max = jnp.maximum(old_max, jnp.max(scores, axis=0, keepdims=True))
                rescale = jnp.exp2((old_max - new_max) * scale)
                weights = jnp.exp2((scores - new_max) * scale)
                if masked:
                    weights = jnp.where(visible, weights, 0.0)
                sums = jnp.sum(weights, axis=0, keepdims=True)
                mixed = jnp.dot(vals_t, weights.astype(jnp.bfloat16), preferred_element_type=jnp.float32)
                l_ref[...] = rescale * l_ref[...] + sums
                acc_ref[...] = rescale * acc_ref[...] + mixed
                m_ref[...] = new_max

        block(own, True)

        def masked_step(p, carry, block=block):
            block(p, True)
            return carry

        def full_step(p, carry, block=block):
            block(p, False)
            return carry

        lax.fori_loop(low, full_low, masked_step, 0)
        lax.fori_loop(jnp.maximum(full_low, low), own, full_step, 0)

        if last:
            out_t = acc_ref[...] / l_ref[...]
            for h in range(heads):
                o_ref[j * span_len:(j + 1) * span_len, h * HEAD_DIM:(h + 1) * HEAD_DIM] = out_t[
                    :, h * span_len:(h + 1) * span_len
                ].astype(o_ref.dtype).T


def span_blocks(keys, vals, span_len):
    n = keys.shape[0] // span_len
    vals_t = jnp.swapaxes(vals.reshape(n, span_len, HEAD_DIM), 1, 2)
    return jnp.concatenate([keys.reshape(n, span_len, HEAD_DIM), vals_t], axis=2)


def attend_all(queries, key_rows, value_rows, span_order, doc_start):
    tok_rows = queries.shape[0]
    heads = queries.shape[1] // HEAD_DIM
    kv_count = key_rows.shape[1] // HEAD_DIM
    n_ctx = lax.axis_size("ctx")
    n_head = lax.axis_size("head")
    n_dev = n_ctx * n_head
    ctx_index = lax.axis_index("ctx")
    n_spans = span_order.shape[0]
    length = key_rows.shape[0] * n_dev
    span_len = length // n_spans
    n_local = tok_rows // span_len
    group_index = lax.axis_index("head") * kv_count // n_head
    slot_ids = jnp.arange(n_spans, dtype=jnp.int32)

    if kv_count == 1 and n_dev == 32 and key_rows.shape[0] == span_len:
        flat_index = ctx_index * n_head + lax.axis_index("head")
        local = span_blocks(key_rows, value_rows, span_len)
        pieces, source = doubling_gather(local, flat_index, n_dev)
    else:
        both = jnp.concatenate([key_rows, value_rows], axis=1)
        block_rows = lax.all_gather(both, "head", axis=0, tiled=True)
        own_keys = lax.dynamic_slice_in_dim(block_rows, group_index * HEAD_DIM, HEAD_DIM, 1)
        own_vals = lax.dynamic_slice_in_dim(
            block_rows, (kv_count + group_index) * HEAD_DIM, HEAD_DIM, 1
        )
        local = span_blocks(own_keys, own_vals, span_len)
        whole = lax.all_gather(local, "ctx", axis=0, tiled=True)
        pieces = [whole]
        source = slot_ids

    inverse = jnp.sum(
        jnp.where(span_order[None, :] == slot_ids[:, None], slot_ids[None, :], 0), axis=1
    ).astype(jnp.int32)
    where_held = jnp.sum(
        jnp.where(inverse[:, None] == source[None, :], slot_ids[None, :], 0), axis=1
    ).astype(jnp.int32)

    local_slots = ctx_index * n_local + jnp.arange(n_local, dtype=jnp.int32)
    own_span = jnp.sum(
        jnp.where(local_slots[:, None] == slot_ids[None, :], span_order[None, :], 0), axis=1
    ).astype(jnp.int32)
    doc_spans = doc_start.reshape(n_local, span_len)
    low = jnp.min(doc_spans, axis=1) // span_len
    full_low = (jnp.max(doc_spans, axis=1) + span_len - 1) // span_len
    info = jnp.stack([own_span, low, full_low]).astype(jnp.int32)

    rows = heads * span_len
    doc_rows = doc_start.reshape(n_local, 1, span_len)
    q_t = jnp.transpose(
        queries.reshape(n_local, span_len, heads, HEAD_DIM), (0, 3, 2, 1)
    ).reshape(n_local, HEAD_DIM, rows)

    blocks_est = n_local * (n_spans // 2 + 1)
    state_shapes = [
        jax.ShapeDtypeStruct((n_local, 1, rows), jnp.float32),
        jax.ShapeDtypeStruct((n_local, 1, rows), jnp.float32),
        jax.ShapeDtypeStruct((n_local, HEAD_DIM, rows), jnp.float32),
    ]
    out_shape = jax.ShapeDtypeStruct(queries.shape, queries.dtype)
    vmem = pl.BlockSpec(memory_space=pltpu.VMEM)
    smem = pl.BlockSpec(memory_space=pltpu.SMEM)
    state = None
    base = 0
    for index, piece in enumerate(pieces):
        first = index == 0
        last = index == len(pieces) - 1
        piece = tuple(piece) if isinstance(piece, tuple) else (piece,)
        n_blocks = sum(x.shape[0] for x in piece)
        share = n_blocks / n_spans
        kernel = functools.partial(
            attend_kernel, heads=heads, span_len=span_len, scale=HEAD_DIM ** (-0.5) * LOG2_E,
            base=base, first=first, last=last, n_local=n_local, n_kv=len(piece),
        )
        cost = pl.CostEstimate(
            flops=int(4 * rows * span_len * HEAD_DIM * blocks_est * share),
            transcendentals=int(rows * span_len * blocks_est * share),
            bytes_accessed=2 * queries.size * 2 + n_blocks * span_len * 4 * HEAD_DIM,
        )
        operands = [info, where_held, q_t, *piece, doc_rows]
        in_specs = [smem, smem, vmem] + [vmem] * len(piece) + [vmem]
        if not first:
            operands = operands + list(state)
            in_specs = in_specs + [vmem] * 3
        out_shapes = list(state_shapes) + ([out_shape] if last else [])
        result = pl.pallas_call(
            kernel,
            in_specs=in_specs,
            out_specs=[vmem] * len(out_shapes),
            out_shape=out_shapes,
            cost_estimate=cost,
        )(*operands)
        base += n_blocks
        if last:
            return result[3]
        state = result[:3]


def solution(mesh):
    in_specs = (P("ctx", "head"), P(("ctx", "head"), None), P(("ctx", "head"), None), P(), P("ctx"))
    out_specs = P("ctx", "head")
    return jax.shard_map(
        attend_all, mesh=mesh, in_specs=in_specs, out_specs=out_specs, check_vma=False
    )
```

```python
import functools

import jax
import jax.numpy as jnp
from jax import lax
from jax.experimental import pallas as pl
from jax.experimental.pallas import tpu as pltpu
from jax.sharding import PartitionSpec as P


HEAD_DIM = 128


NEG = -1e30
START_MAX = -1e29
LOG2_E = 1.4426950408889634

ORDER_CORE0 = (4, 3, 2, 0)
ORDER_CORE1 = (0, 2, 4, 3)
CORE_BIT = 1


def doubling_gather(block, flat_index, n_dev):
    core = (flat_index >> CORE_BIT) & 1
    held = block
    pieces = []
    for step in range(len(ORDER_CORE0)):
        pairs = []
        for k in range(n_dev):
            bit = ORDER_CORE0[step] if ((k >> CORE_BIT) & 1) == 0 else ORDER_CORE1[step]
            pairs.append((k, k ^ (1 << bit)))
        other = lax.ppermute(held, ("ctx", "head"), pairs)
        if step == len(ORDER_CORE0) - 1:
            pieces.append(held)
            pieces.append(other)
            held = (held, other)
        else:
            held = jnp.concatenate([held, other], axis=0)
    other = lax.ppermute(held, ("ctx", "head"), [(k, k ^ (1 << CORE_BIT)) for k in range(n_dev)])
    pieces.append(tuple(other))

    def source_mask(order, j):
        mask = 0
        for t, bit in enumerate(order):
            mask = mask | (((j >> t) & 1) << bit)
        return mask

    half = 1 << len(ORDER_CORE0)
    j = jnp.arange(2 * half, dtype=jnp.int32)
    jl = j % half
    own_order_mask = jnp.where(core == 0, source_mask(ORDER_CORE0, jl), source_mask(ORDER_CORE1, jl))
    partner_order_mask = jnp.where(
        core == 0, source_mask(ORDER_CORE1, jl), source_mask(ORDER_CORE0, jl)
    )
    partner = flat_index ^ (1 << CORE_BIT)
    source = jnp.where(j < half, flat_index ^ own_order_mask, partner ^ partner_order_mask)
    return pieces, source


def attend_kernel(info_ref, slot_ref, qt_ref, *rest,
                  heads, span_len, scale, base, first, last, n_local, n_kv):
    rest = list(rest)
    kv_refs = rest[:n_kv]
    doc_ref = rest[n_kv]
    rest = rest[n_kv + 1:]
    if not first:
        im_all, il_all, iacc_all = rest[:3]
        rest = rest[3:]
    m_all, l_all, acc_all = rest[:3]
    o_ref = rest[3] if last else None
    count = sum(r.shape[0] for r in kv_refs)

    def load_kv(b):
        kv = kv_refs[0][jnp.minimum(b, kv_refs[0].shape[0] - 1)]
        offset = kv_refs[0].shape[0]
        for r in kv_refs[1:]:
            here = r[jnp.clip(b - offset, 0, r.shape[0] - 1)]
            kv = jnp.where(b >= offset, here, kv)
            offset += r.shape[0]
        return kv

    rows = heads * span_len
    cols = lax.broadcasted_iota(jnp.int32, (1, rows), 1)

    for j in range(n_local):
        own = info_ref[0, j]
        low = info_ref[1, j]
        full_low = jnp.minimum(info_ref[2, j], own)
        m_ref = m_all.at[j]
        l_ref = l_all.at[j]
        acc_ref = acc_all.at[j]
        qt_ref_j = qt_ref.at[j]

        if first:
            m_ref[...] = jnp.full(m_ref.shape, START_MAX, jnp.float32)
            l_ref[...] = jnp.zeros(l_ref.shape, jnp.float32)
            acc_ref[...] = jnp.zeros(acc_ref.shape, jnp.float32)
        else:
            m_ref[...] = im_all[j]
            l_ref[...] = il_all[j]
            acc_ref[...] = iacc_all[j]

        doc = jnp.concatenate([doc_ref[j]] * heads, axis=1)
        qpos = own * span_len + lax.rem(cols, span_len)

        def block(p, masked, m_ref=m_ref, l_ref=l_ref, acc_ref=acc_ref, qt_ref_j=qt_ref_j,
                  doc=doc, qpos=qpos):
            b = slot_ref[p] - base

            @pl.when((b >= 0) & (b < count))
            def _():
                kv = load_kv(b)
                keys = kv[:, :HEAD_DIM]
                vals_t = kv[:, HEAD_DIM:]
                scores = jnp.dot(keys, qt_ref_j[...], preferred_element_type=jnp.float32)
                if masked:
                    kpos = p * span_len + lax.broadcasted_iota(jnp.int32, (span_len, 1), 0)
                    visible = (kpos >= doc) & (kpos <= qpos)
                    scores = jnp.where(visible, scores, NEG)
                old_max = m_ref[...]
                new_max = jnp.maximum(old_max, jnp.max(scores, axis=0, keepdims=True))
                rescale = jnp.exp2((old_max - new_max) * scale)
                weights = jnp.exp2((scores - new_max) * scale)
                sums = jnp.sum(weights, axis=0, keepdims=True)
                mixed = jnp.dot(vals_t, weights.astype(jnp.bfloat16), preferred_element_type=jnp.float32)
                l_ref[...] = rescale * l_ref[...] + sums
                acc_ref[...] = rescale * acc_ref[...] + mixed
                m_ref[...] = new_max

        block(own, True)

        def masked_step(p, carry, block=block):
            block(p, True)
            return carry

        def full_step(p, carry, block=block):
            block(p, False)
            return carry

        lax.fori_loop(low, full_low, masked_step, 0)
        lax.fori_loop(jnp.maximum(full_low, low), own, full_step, 0)

        if last:
            out_t = acc_ref[...] / l_ref[...]
            for h in range(heads):
                o_ref[j * span_len:(j + 1) * span_len, h * HEAD_DIM:(h + 1) * HEAD_DIM] = out_t[
                    :, h * span_len:(h + 1) * span_len
                ].astype(o_ref.dtype).T


def span_blocks(keys, vals, span_len):
    n = keys.shape[0] // span_len
    vals_t = jnp.swapaxes(vals.reshape(n, span_len, HEAD_DIM), 1, 2)
    return jnp.concatenate([keys.reshape(n, span_len, HEAD_DIM), vals_t], axis=2)


def attend_all(queries, key_rows, value_rows, span_order, doc_start):
    tok_rows = queries.shape[0]
    heads = queries.shape[1] // HEAD_DIM
    kv_count = key_rows.shape[1] // HEAD_DIM
    n_ctx = lax.axis_size("ctx")
    n_head = lax.axis_size("head")
    n_dev = n_ctx * n_head
    ctx_index = lax.axis_index("ctx")
    n_spans = span_order.shape[0]
    length = key_rows.shape[0] * n_dev
    span_len = length // n_spans
    n_local = tok_rows // span_len
    group_index = lax.axis_index("head") * kv_count // n_head
    slot_ids = jnp.arange(n_spans, dtype=jnp.int32)

    if kv_count == 1 and n_dev == 32 and key_rows.shape[0] == span_len:
        flat_index = ctx_index * n_head + lax.axis_index("head")
        local = span_blocks(key_rows, value_rows, span_len)
        pieces, source = doubling_gather(local, flat_index, n_dev)
    else:
        both = jnp.concatenate([key_rows, value_rows], axis=1)
        block_rows = lax.all_gather(both, "head", axis=0, tiled=True)
        own_keys = lax.dynamic_slice_in_dim(block_rows, group_index * HEAD_DIM, HEAD_DIM, 1)
        own_vals = lax.dynamic_slice_in_dim(
            block_rows, (kv_count + group_index) * HEAD_DIM, HEAD_DIM, 1
        )
        local = span_blocks(own_keys, own_vals, span_len)
        whole = lax.all_gather(local, "ctx", axis=0, tiled=True)
        pieces = [whole]
        source = slot_ids

    inverse = jnp.sum(
        jnp.where(span_order[None, :] == slot_ids[:, None], slot_ids[None, :], 0), axis=1
    ).astype(jnp.int32)
    where_held = jnp.sum(
        jnp.where(inverse[:, None] == source[None, :], slot_ids[None, :], 0), axis=1
    ).astype(jnp.int32)

    local_slots = ctx_index * n_local + jnp.arange(n_local, dtype=jnp.int32)
    own_span = jnp.sum(
        jnp.where(local_slots[:, None] == slot_ids[None, :], span_order[None, :], 0), axis=1
    ).astype(jnp.int32)
    doc_spans = doc_start.reshape(n_local, span_len)
    low = jnp.min(doc_spans, axis=1) // span_len
    full_low = (jnp.max(doc_spans, axis=1) + span_len - 1) // span_len
    info = jnp.stack([own_span, low, full_low]).astype(jnp.int32)

    rows = heads * span_len
    doc_rows = doc_start.reshape(n_local, 1, span_len)
    q_t = jnp.transpose(
        queries.reshape(n_local, span_len, heads, HEAD_DIM), (0, 3, 2, 1)
    ).reshape(n_local, HEAD_DIM, rows)

    blocks_est = n_local * (n_spans // 2 + 1)
    state_shapes = [
        jax.ShapeDtypeStruct((n_local, 1, rows), jnp.float32),
        jax.ShapeDtypeStruct((n_local, 1, rows), jnp.float32),
        jax.ShapeDtypeStruct((n_local, HEAD_DIM, rows), jnp.float32),
    ]
    out_shape = jax.ShapeDtypeStruct(queries.shape, queries.dtype)
    vmem = pl.BlockSpec(memory_space=pltpu.VMEM)
    smem = pl.BlockSpec(memory_space=pltpu.SMEM)
    state = None
    base = 0
    for index, piece in enumerate(pieces):
        first = index == 0
        last = index == len(pieces) - 1
        piece = tuple(piece) if isinstance(piece, tuple) else (piece,)
        n_blocks = sum(x.shape[0] for x in piece)
        share = n_blocks / n_spans
        kernel = functools.partial(
            attend_kernel, heads=heads, span_len=span_len, scale=HEAD_DIM ** (-0.5) * LOG2_E,
            base=base, first=first, last=last, n_local=n_local, n_kv=len(piece),
        )
        cost = pl.CostEstimate(
            flops=int(4 * rows * span_len * HEAD_DIM * blocks_est * share),
            transcendentals=int(rows * span_len * blocks_est * share),
            bytes_accessed=2 * queries.size * 2 + n_blocks * span_len * 4 * HEAD_DIM,
        )
        operands = [info, where_held, q_t, *piece, doc_rows]
        in_specs = [smem, smem, vmem] + [vmem] * len(piece) + [vmem]
        if not first:
            operands = operands + list(state)
            in_specs = in_specs + [vmem] * 3
        out_shapes = list(state_shapes) + ([out_shape] if last else [])
        result = pl.pallas_call(
            kernel,
            in_specs=in_specs,
            out_specs=[vmem] * len(out_shapes),
            out_shape=out_shapes,
            cost_estimate=cost,
        )(*operands)
        base += n_blocks
        if last:
            return result[3]
        state = result[:3]


def solution(mesh):
    in_specs = (P("ctx", "head"), P(("ctx", "head"), None), P(("ctx", "head"), None), P(), P("ctx"))
    out_specs = P("ctx", "head")
    return jax.shard_map(
        attend_all, mesh=mesh, in_specs=in_specs, out_specs=out_specs, check_vma=False
    )
```
